128 devices in a mesh: ctx: 16 (over y, x), grp: 8 (over z, core).
Axes of the slice: x: 4, y: 4, z: 4, core: 2. Of those that a mesh axis runs over, the one named last changes fastest.
Arguments:
- residual: bfloat16 [8, 2048, 2880], P('grp', 'ctx'), may hold values from -3 to 3
- queries: bfloat16 [8, 2048, 2048], P('grp', 'ctx'), may hold values from -8 to 8
- stretch_kv: bfloat16 [8, 2048, 1024], P('grp', 'ctx'), may hold values from -8 to 8
- cache_kv: bfloat16 [8, 4096, 1024], P('grp', 'ctx'), may hold values from -6 to 6
- doc_lengths: int32 [8, 8], P('grp'), may hold values from 1 to 3072, 6144 in all within a row
- sinks: float32 [32], replicated, may hold values from 2 to 6
- out_proj: bfloat16 [2048, 2880], P('ctx'), may hold values from -0.75 to 0.75
- norm_gain: float32 [2880], replicated, may hold values from 0.1 to 1.9
- router: bfloat16 [2880, 64], replicated, may hold values from -0.109375 to 0.109375
- expert_ids: int32 [8, 2048, 4], P('grp', 'ctx'), may hold values from 0 to 63, all different within a row; in each aligned block of 128 rows (0 to 127, 128 to 255, ..., all dimensions but the last counted through in order) at most 10 rows name the same one
- expert_in: bfloat16 [128, 2880, 1536], P(('ctx', 'grp')), may hold values from -0.109375 to 0.109375
- expert_out: bfloat16 [128, 768, 2880], P(('ctx', 'grp')), may hold values from -0.15625 to 0.15625
Outputs:
- resid_mid: bfloat16 [8, 2048, 2880], P('grp', 'ctx')
- layer_out: bfloat16 [8, 2048, 2880], P('grp', 'ctx')
The draws below stay inside these ranges and needn't reach their ends.
Inputs may be any that keep to these rules, and one draw needn't show every extreme that they name: `expert_ids`: in the rows of one device (aligned blocks of 128 tokens, sequence after sequence), each expert is named by at most 10 rows, and in some blocks one expert by exactly 10; a token's 4 experts differ. `doc_lengths`: A sequence's 8 lengths sum to 6144; the longest is exactly 3072.
All inputs are finite; a program needn't handle non-finite values.
Results may differ from the reference program's by a relative error of at most 0.015.
Values may be sent and summed in bfloat16 or wider, within the bound.
No kernel may reach another device: no remote copies, remote signals or barrier semaphores. Data moves between devices by JAX's collectives and lax.ppermute only.
A program may use at most 128 MiB of HBM per device.

```python
import math
import jax
import jax.numpy as jnp
import numpy as np
from jax import lax

D = 2880
HEADS = 32
KVH = 8
HD = 64
EXP_HID = 1536
HALF = 768
TOPK = 4
NDOCS = 8
TOK_DEV = 128
SEQS = 8
STRETCH = 2048
CACHE = 4096
LENGTH = 6144
EXPERTS = 64
OWNERS = 128
CAP = 10
N_CTX = 16
N_GRP = 8


def draw_queries(key, part):
    shape = (SEQS, STRETCH, HEADS * HD)
    values = jax.random.truncated_normal(jax.random.fold_in(key, 11), -6.0, 6.0, shape, jnp.float32)
    return values.astype(jnp.bfloat16)


def draw_stretch_kv(key, part):
    shape = (SEQS, STRETCH, 2 * KVH * HD)
    values = jax.random.truncated_normal(jax.random.fold_in(key, 21), -6.0, 6.0, shape, jnp.float32)
    return values.astype(jnp.bfloat16)


def steps_of(own_key, shape, split, smallest, high):
    def one(dim, parts):
        steps = jax.random.uniform(jax.random.fold_in(jax.random.fold_in(own_key, 6), dim), (parts,), jnp.float32, smallest / len(split), high / len(split))
        return jnp.repeat(jnp.exp(steps), shape[dim] // parts).reshape((-1,) + (1,) * (len(shape) - dim - 1))

    level = one(*split[0])
    for cut in split[1:]:
        level = level * one(*cut)
    return level


def split_up(count, total, most, slope):
    loads = [(1 << 20) // math.isqrt(grade ** slope) + 1 for grade in range(2, count + 1)]
    spare, given = total - most - (count - 1), [1] * (count - 1)
    while spare > 0:
        free = [i for i in range(count - 1) if given[i] < most]
        whole, remaining = sum([loads[i] for i in free]), spare
        for i in free:
            more = min(most - given[i], max(1, remaining * loads[i] // whole), spare)
            given[i] = given[i] + more
            spare = spare - more
    return np.array([most] + given)


def uneven_parts(key, amount, total, limit, skew):
    if amount == 2:
        one = jax.random.randint(key, (), max(1, total - limit), min(limit, total - 1) + 1)
        return jnp.stack([one, total - one])
    sizes = jnp.asarray(split_up(amount, total, limit, skew), jnp.int32)
    pairs = (amount - 1) // 2
    donor, sink = sizes[1:1 + 2 * pairs:2], sizes[2:2 + 2 * pairs:2]
    slack = jnp.minimum(donor - 1, limit - sink)
    shifted = jax.random.randint(jax.random.fold_in(key, 1), (pairs,), 0, 1 << 20) % (slack + 1)
    sizes = sizes.at[1:1 + 2 * pairs:2].set(donor - shifted).at[2:2 + 2 * pairs:2].set(sink + shifted)
    return sizes[jax.random.permutation(jax.random.fold_in(key, 2), amount)]


def routed_block(own_key, own, number, rows, number_of, top, limit, lean):
    order = jax.random.permutation(own_key, number_of)
    heavy_load, ordinary = shares(number_of, rows * top, limit, lean, True), shares(number_of, rows * top, limit, lean, False)
    places = jnp.arange(number_of)

    def named(tallies, turn):
        used = int((tallies > 0).sum())
        fixed = max(1, used // 4)
        shifted = fixed + (places - fixed + turn * (used - fixed)) % max(1, number_of - fixed)
        return jnp.zeros((number_of,), jnp.int32).at[order[jnp.where(places < fixed, places, shifted)]].set(jnp.asarray(tallies, jnp.int32))

    tallies = jnp.where(number % 4 == 0, named(heavy_load, number // 4), named(ordinary, number - number // 4 - 1))
    mixed = jax.random.permutation(jax.random.fold_in(own, 3), number_of)
    source_of, sink = mixed[0:number_of // 2 * 2:2], mixed[1:number_of // 2 * 2:2]
    margin = jnp.minimum(tallies[source_of] - 1, limit - tallies[sink]) // 2
    margin = jnp.where((source_of == order[0]) | (sink == order[0]) | (tallies[sink] == 0), 0, jnp.maximum(margin, 0))
    shifted = jax.random.randint(jax.random.fold_in(own, 4), (number_of // 2,), 0, 1 << 20) % (margin + 1)
    tallies = tallies.at[source_of].add(-shifted).at[sink].add(shifted)
    items = jnp.searchsorted(jnp.cumsum(tallies), jnp.arange(rows * top), side="right").astype(jnp.int32)
    listing = items.reshape(top, rows).T
    listing = listing[jax.random.permutation(jax.random.fold_in(own, 1), rows)]
    turn = jax.random.randint(jax.random.fold_in(own, 2), (rows, 1), 0, top)
    return jnp.take_along_axis(listing, (jnp.arange(top)[None, :] + turn) % top, axis=1)


def shares(number_of, total, reach, skew, full):
    weights = [(1 << 20) // math.isqrt(grade ** skew) + 1 for grade in range(1, number_of + 1)]
    largest = reach if full else min(reach, max(-(-total // number_of), total * weights[0] // sum(weights)))
    least = 1 if total - largest >= number_of - 1 else 0
    holding, spare = [largest] + [least] * (number_of - 1), total - largest - least * (number_of - 1)
    while spare > 0:
        movable = [i for i in range(1, number_of) if holding[i] < largest] or [i for i in range(1, number_of) if holding[i] < reach]
        whole, left = sum([weights[i] for i in movable]), spare
        for i in movable:
            addition = min(reach - holding[i], max(1, left * weights[i] // whole), spare)
            holding[i] = holding[i] + addition
            spare = spare - addition
    return np.array(holding)


def bell_draw(key, extent, width, most, shards=(), kind=jnp.bfloat16):
    loudness = steps_of(key, extent, shards, -0.22, 0.18) if shards else 1.0
    drawn = jax.random.normal(key, extent, jnp.float32) * width * loudness
    return jnp.minimum(jnp.maximum(drawn, -most), most).astype(kind)


def setup_inputs(seed: int = 0) -> dict:
    key_list = jax.random.split(jax.random.key(seed), 13)
    residual = bell_draw(key_list[0], (SEQS, STRETCH, D), 0.5, 3.0, ((0, 8), (1, 16)))
    queries = draw_queries(jax.random.fold_in(key_list[12], 71), 0)
    stretch_kv = draw_stretch_kv(jax.random.fold_in(key_list[12], 71), 0)
    cache_kv = bell_draw(key_list[3], (SEQS, CACHE, 2 * KVH * HD), 1.0, 6.0, ((0, 8), (1, 16)))
    doc_lengths = jax.vmap(lambda own: uneven_parts(own, NDOCS, LENGTH, LENGTH // 2, 1))(jax.random.split(key_list[4], SEQS)).reshape((SEQS, NDOCS)).astype(jnp.int32)
    sinks = jnp.clip(jax.random.uniform(key_list[5], (HEADS,), jnp.float32, 2.0, 6.0), 2.0, 6.0)
    out_proj = bell_draw(key_list[6], (HEADS * HD, D), 0.125, 0.75, ((0, 16),))
    norm_gain = jnp.clip(1.0 + 0.18 * jax.random.normal(key_list[7], (D,), jnp.float32), 0.1, 1.9)
    router = bell_draw(key_list[8], (D, EXPERTS), D ** -0.5, 0.109375)
    expert_ids_keys = jax.random.split(jax.random.fold_in(key_list[9], 1), SEQS * STRETCH // TOK_DEV)
    expert_ids_turns = jax.random.permutation(jax.random.fold_in(key_list[9], 3), SEQS * STRETCH // TOK_DEV)
    expert_ids = jax.vmap(lambda own, number: routed_block(jax.random.fold_in(key_list[9], 2), own, number, TOK_DEV, EXPERTS, TOPK, CAP, 1))(expert_ids_keys, expert_ids_turns).reshape((SEQS, STRETCH, TOPK))
    expert_in = bell_draw(key_list[10], (OWNERS, D, EXP_HID), D ** -0.5, 0.109375, ((0, 128),))
    expert_out = bell_draw(key_list[11], (OWNERS, HALF, D), EXP_HID ** -0.5, 0.15625, ((0, 128),))
    return dict(residual=residual, queries=queries, stretch_kv=stretch_kv, cache_kv=cache_kv, doc_lengths=doc_lengths, sinks=sinks, out_proj=out_proj, norm_gain=norm_gain, router=router, expert_ids=expert_ids, expert_in=expert_in, expert_out=expert_out)


def doc_index(positions, lengths):
    ends = jnp.cumsum(lengths)
    return lax.optimization_barrier(jnp.sum((positions[:, None] >= ends[None, :]).astype(jnp.int32), axis=1))

def gated_act(pre, half_width):
    gate = pre[:, :half_width]
    upper = pre[:, half_width:]
    return ((upper + 1.0) * gate * jax.nn.sigmoid(1.702 * gate)).astype(jnp.bfloat16)

def reference(residual, queries, stretch_kv, cache_kv, doc_lengths, sinks, out_proj, norm_gain, router, expert_ids, expert_in, expert_out):
    groups = HEADS // KVH
    kv_cols = KVH * HD
    block = math.gcd(STRETCH, 512)
    scale = 1.0 / math.sqrt(HD)
    sink_grid = sinks.reshape(KVH, groups).astype(jnp.float32)
    key_pos = jnp.arange(LENGTH, dtype=jnp.int32)

    def one_sequence(inputs):
        seq_queries, seq_stretch, seq_cache, seq_lengths = inputs
        joined = jnp.concatenate([seq_cache, seq_stretch], axis=0)
        keys = joined[:, :kv_cols].reshape(LENGTH, KVH, HD).astype(jnp.float32)
        values = joined[:, kv_cols:].reshape(LENGTH, KVH, HD).astype(jnp.float32)
        key_doc = doc_index(key_pos, seq_lengths)

        def one_block(index):
            first = (index * block).astype(jnp.int32)
            part = lax.dynamic_slice_in_dim(seq_queries, first, block, 0)
            part = part.reshape(block, KVH, groups, HD).astype(jnp.float32)
            query_pos = CACHE + first + jnp.arange(block, dtype=jnp.int32)
            query_doc = doc_index(query_pos, seq_lengths)
            allowed = (key_pos[None, :] <= query_pos[:, None]) & (key_doc[None, :] == query_doc[:, None])
            scores = jnp.einsum('qkgd,skd->kgqs', part, keys) * scale
            masked = jnp.where(allowed[None, None], scores, -jnp.inf)
            top = jnp.maximum(lax.optimization_barrier(jnp.max(masked, axis=-1)), sink_grid[:, :, None])
            weights = jnp.where(allowed[None, None], jnp.exp(scores - top[..., None]), 0.0)
            denom = lax.optimization_barrier(jnp.sum(weights, axis=-1)) + jnp.exp(sink_grid[:, :, None] - top)
            rounded = lax.optimization_barrier(weights.astype(jnp.bfloat16))
            numer = jnp.einsum('kgqs,skd->kgqd', rounded.astype(jnp.float32), values)
            result = numer / denom[..., None]
            return jnp.transpose(result, (2, 0, 1, 3)).reshape(block, HEADS * HD).astype(jnp.bfloat16)
        blocks = lax.map(one_block, jnp.arange(STRETCH // block, dtype=jnp.int32))
        return blocks.reshape(STRETCH, HEADS * HD)
    attended = lax.map(one_sequence, (queries, stretch_kv, cache_kv, doc_lengths))
    projected = jnp.dot(attended.reshape(-1, HEADS * HD), out_proj, preferred_element_type=jnp.float32)
    mid = (residual.reshape(-1, D).astype(jnp.float32) + projected).astype(jnp.bfloat16)
    mid_float = mid.astype(jnp.float32)
    normed = (mid_float * lax.rsqrt(lax.optimization_barrier(jnp.mean(mid_float * mid_float, axis=-1, keepdims=True)) + 1e-05) * norm_gain).astype(jnp.bfloat16)
    logits = jnp.dot(normed, router, preferred_element_type=jnp.float32)
    chosen_ids = expert_ids.reshape(-1, TOPK)
    picks = chosen_ids[:, :, None] == jnp.arange(EXPERTS, dtype=jnp.int32)[None, None, :]
    chosen = lax.optimization_barrier(jnp.sum(jnp.where(picks, logits[:, None, :], 0.0), axis=-1))
    raised = jnp.exp(chosen)
    route_weights = raised / lax.optimization_barrier(jnp.sum(raised, axis=-1, keepdims=True))
    flat_ids = chosen_ids.reshape(-1)
    weights_flat = route_weights.reshape(-1)
    most_rows = min(N_CTX * N_GRP * CAP, flat_ids.shape[0])

    def add_expert(index, total):
        order = jnp.argsort((flat_ids != index).astype(jnp.int32), stable=True)[:most_rows]
        token_rows = order // TOPK
        live = flat_ids[order] == index
        rows = normed[token_rows]
        summed = jnp.zeros((most_rows, D), jnp.float32)
        for half_index in range(2):
            owner = (2 * index + half_index).astype(jnp.int32)
            first_w = lax.dynamic_index_in_dim(expert_in, owner, 0, keepdims=False)
            second_w = lax.dynamic_index_in_dim(expert_out, owner, 0, keepdims=False)
            pre = jnp.dot(rows, first_w, preferred_element_type=jnp.float32)
            hidden = gated_act(pre, HALF)
            part_out = jnp.dot(hidden, second_w, preferred_element_type=jnp.float32).astype(jnp.bfloat16)
            summed = summed + part_out.astype(jnp.float32)
        rounded_rows = lax.optimization_barrier(summed.astype(jnp.bfloat16))
        contrib = rounded_rows.astype(jnp.float32) * jnp.where(live, weights_flat[order], 0.0)[:, None]
        return total.at[token_rows].add(contrib)
    mixture = lax.fori_loop(0, EXPERTS, add_expert, jnp.zeros((flat_ids.shape[0] // TOPK, D), jnp.float32))
    final = (mid_float + mixture).astype(jnp.bfloat16)
    return (mid.reshape(SEQS, STRETCH, D), final.reshape(SEQS, STRETCH, D))
```

```python
import math

import jax
import jax.numpy as jnp
from jax import lax
from jax.sharding import PartitionSpec as P

HEADS = 32
KVH = 8
HD = 64


def doc_index(positions, lengths):
    ends = jnp.cumsum(lengths)
    return jnp.sum((positions[:, None] >= ends[None, :]).astype(jnp.int32), axis=1)


def gated_act(pre, half_width):
    gate = pre[:, :half_width]
    upper = pre[:, half_width:]
    return ((upper + 1.0) * gate * jax.nn.sigmoid(1.702 * gate)).astype(jnp.bfloat16)


def body(
    residual,
    queries,
    stretch_kv,
    cache_kv,
    doc_lengths,
    sinks,
    out_proj,
    norm_gain,
    router,
    expert_ids,
    expert_in,
    expert_out,
):
    tokens = residual.shape[1]
    width = residual.shape[2]
    cache_rows = cache_kv.shape[1]
    kv_cols = stretch_kv.shape[2] // 2
    groups = HEADS // KVH
    ctx_count = lax.axis_size("ctx")
    ctx_here = lax.axis_index("ctx")
    stretch_base = cache_rows * ctx_count
    span = cache_rows + tokens
    query_pos = stretch_base + ctx_here * tokens + jnp.arange(tokens, dtype=jnp.int32)
    lengths = doc_lengths[0]
    query_doc = doc_index(query_pos, lengths)
    query_heads = queries[0].reshape(tokens, KVH, groups, HD)
    sink_grid = sinks.reshape(KVH, groups)
    local_kv = jnp.concatenate([cache_kv[0], stretch_kv[0]], axis=0)
    scale = 1.0 / math.sqrt(HD)

    def key_block(carry, keys_values, first):
        count = keys_values.shape[0]
        rows = first + jnp.arange(count, dtype=jnp.int32)
        source = rows // span
        offset = rows % span
        key_pos = jnp.where(
            offset < cache_rows,
            source * cache_rows + offset,
            stretch_base + source * tokens + offset - cache_rows,
        )
        key_doc = doc_index(key_pos, lengths)
        allowed = (key_pos[None, :] <= query_pos[:, None]) & (
            key_doc[None, :] == query_doc[:, None]
        )
        keys = keys_values[:, :kv_cols].reshape(count, KVH, HD)
        values = keys_values[:, kv_cols:].reshape(count, KVH, HD)
        top, total, numer = carry
        scores = (
            jnp.einsum("qkgd,skd->kgqs", query_heads, keys, preferred_element_type=jnp.float32)
            * scale
        )
        masked = jnp.where(allowed[None, None], scores, -jnp.inf)
        new_top = jnp.maximum(top, jnp.max(masked, axis=-1))
        weights = jnp.where(allowed[None, None], jnp.exp(scores - new_top[..., None]), 0.0)
        shrink = jnp.exp(top - new_top)
        total = total * shrink + jnp.sum(weights, axis=-1)
        numer = numer * shrink[..., None] + jnp.einsum(
            "kgqs,skd->kgqd",
            weights.astype(jnp.bfloat16),
            values,
            preferred_element_type=jnp.float32,
        )
        return (new_top, total, numer)

    start_top = jnp.broadcast_to(sink_grid[:, :, None], (KVH, groups, tokens))
    start_total = jnp.zeros((KVH, groups, tokens), jnp.float32)
    start_numer = jnp.zeros((KVH, groups, tokens, HD), jnp.float32)
    piece = lax.all_gather(local_kv, "ctx", axis=0, tiled=True)
    count = piece.shape[0]
    step_rows = math.gcd(count, 1024)

    def advance(index, state):
        first = index * step_rows
        part = lax.dynamic_slice_in_dim(piece, first, step_rows, 0)
        return key_block(state, part, first)

    top, total, numer = lax.fori_loop(
        0, count // step_rows, advance, (start_top, start_total, start_numer)
    )
    denom = total + jnp.exp(sink_grid[:, :, None] - top)
    attended = (
        jnp.transpose(numer / denom[..., None], (2, 0, 1, 3))
        .reshape(tokens, HEADS * HD)
        .astype(jnp.bfloat16)
    )
    grp_here = lax.axis_index("grp")
    parity = grp_here % 2
    grp_count = lax.axis_size("grp")
    pair_perm = [(g, g ^ 1) for g in range(grp_count)]
    head_rows = out_proj.shape[0] // 2
    proj_half = lax.all_gather(
        lax.dynamic_slice_in_dim(out_proj, parity * head_rows, head_rows, 0), "ctx", axis=0, tiled=True
    )
    by_parity = attended.reshape(tokens, HEADS // 2, 2, HD)
    mine = jnp.where(parity == 0, by_parity[:, :, 0], by_parity[:, :, 1]).reshape(tokens, -1)
    theirs_cols = jnp.where(parity == 0, by_parity[:, :, 1], by_parity[:, :, 0]).reshape(tokens, -1)
    partner_cols = lax.ppermute(theirs_cols, "grp", pair_perm)
    both = jnp.dot(
        jnp.concatenate([mine, partner_cols], axis=0), proj_half, preferred_element_type=jnp.float32
    )
    back = lax.ppermute(both[tokens:], "grp", pair_perm)
    projected = both[:tokens] + back
    mid = (residual[0].astype(jnp.float32) + projected).astype(jnp.bfloat16)
    mid_float = mid.astype(jnp.float32)
    normed = (
        mid_float
        * lax.rsqrt(jnp.mean(mid_float * mid_float, axis=-1, keepdims=True) + 1e-05)
        * norm_gain
    ).astype(jnp.bfloat16)
    logits = jnp.dot(normed, router, preferred_element_type=jnp.float32)
    experts = router.shape[1]
    chosen_ids = expert_ids[0]
    topk = chosen_ids.shape[1]
    picks = chosen_ids[:, :, None] == jnp.arange(experts, dtype=jnp.int32)[None, None, :]
    chosen = jnp.sum(jnp.where(picks, logits[:, None, :], 0.0), axis=-1)
    raised = jnp.exp(chosen)
    route_weights = raised / jnp.sum(raised, axis=-1, keepdims=True)
    capacity = 2 * ((5 * tokens * topk + 8 * experts - 1) // (8 * experts))
    flat_ids = chosen_ids.reshape(-1)
    pairs = flat_ids.shape[0]
    onehot = (flat_ids[:, None] == jnp.arange(experts, dtype=jnp.int32)[None, :]).astype(jnp.int32)
    slots = jnp.sum(onehot * (jnp.cumsum(onehot, axis=0) - 1), axis=1)
    dest = flat_ids * capacity + slots
    source_rows = jnp.arange(pairs, dtype=jnp.int32) // topk
    packed = jnp.zeros((experts * capacity, width), jnp.bfloat16).at[dest].set(normed[source_rows])
    packed = packed.reshape(experts, capacity, width)
    in_weights = expert_in[0]
    out_weights = expert_out[0]
    half_width = out_weights.shape[0]
    owners = 2 * experts
    half_cap = capacity // 2
    split = packed.reshape(owners, half_cap, width)
    received = lax.all_to_all(split, ("ctx", "grp"), split_axis=0, concat_axis=0, tiled=True)
    partner_rows = lax.ppermute(received, "grp", pair_perm)

    def expert_half(rows):
        pre = jnp.dot(rows.reshape(-1, width), in_weights, preferred_element_type=jnp.float32)
        hidden = gated_act(pre, half_width)
        return jnp.dot(hidden, out_weights, preferred_element_type=jnp.float32).astype(jnp.bfloat16)

    own_part = expert_half(received)
    partner_part = expert_half(partner_rows)
    partner_back = lax.ppermute(partner_part, "grp", pair_perm)
    summed = (own_part.astype(jnp.float32) + partner_back.astype(jnp.float32)).astype(jnp.bfloat16)
    returned = lax.all_to_all(
        summed.reshape(owners, half_cap, width), ("ctx", "grp"), split_axis=0, concat_axis=0, tiled=True
    )
    expert_rows = returned.reshape(experts * capacity, width)
    gathered = expert_rows[dest].astype(jnp.float32) * route_weights.reshape(-1)[:, None]
    mixture = jnp.sum(gathered.reshape(tokens, topk, width), axis=1)
    final = (mid_float + mixture).astype(jnp.bfloat16)
    return (mid[None], final[None])


def solution(mesh):
    return jax.shard_map(
        body,
        mesh=mesh,
        in_specs=(
            P("grp", "ctx", None),
            P("grp", "ctx", None),
            P("grp", "ctx", None),
            P("grp", "ctx", None),
            P("grp", None),
            P(),
            P("ctx", None),
            P(),
            P(),
            P("grp", "ctx", None),
            P(("ctx", "grp"), None, None),
            P(("ctx", "grp"), None, None),
        ),
        out_specs=(P("grp", "ctx", None), P("grp", "ctx", None)),
        check_vma=False,
    )
```

```python
import math

import jax
import jax.numpy as jnp
from jax import lax
from jax.experimental import pallas as pl
from jax.experimental.pallas import tpu as pltpu
from jax.sharding import PartitionSpec as P

HEADS = 32
KVH = 8
HD = 64
TK = 512


def flash_pairs(qpad, qpos, qstart, sink_rows, cache_g, stretch_g, bounds, scale):
    pairs, rows, lanes = qpad.shape
    n_cache = cache_g.shape[0] // TK
    n_blocks = n_cache + stretch_g.shape[0] // TK
    v_off = cache_g.shape[1] // lanes // 2

    def block_of(j, s):
        return jnp.minimum(s[0] + j, s[1])

    def kernel(s_ref, q_ref, qpos_ref, qstart_ref, sink_ref, ck_ref, cv_ref, sk_ref, sv_ref, o_ref, m_sc, l_sc, acc_sc):
        j = pl.program_id(1)
        b = s_ref[0] + j

        @pl.when(j == 0)
        def _():
            m_sc[...] = sink_ref[...]
            l_sc[...] = jnp.zeros_like(l_sc)
            acc_sc[...] = jnp.zeros_like(acc_sc)

        def step(k_ref, v_ref):
            s = lax.dot_general(
                q_ref[...], k_ref[...], (((1,), (1,)), ((), ())), preferred_element_type=jnp.float32
            ) * scale
            kpos = b * TK + lax.broadcasted_iota(jnp.int32, (1, TK), 1)
            allowed = (kpos <= qpos_ref[...]) & (kpos >= qstart_ref[...])
            m_prev = m_sc[...]
            m_new = jnp.maximum(m_prev, jnp.max(jnp.where(allowed, s, -jnp.inf), axis=1, keepdims=True))
            p = jnp.where(allowed, jnp.exp(s - m_new), 0.0)
            shrink = jnp.exp(m_prev - m_new)
            l_sc[...] = l_sc[...] * shrink + jnp.sum(p, axis=1, keepdims=True)
            acc_sc[...] = acc_sc[...] * shrink + jnp.dot(
                p.astype(jnp.bfloat16), v_ref[...], preferred_element_type=jnp.float32
            )
            m_sc[...] = m_new

        live = b <= s_ref[1]

        @pl.when(live & (b < n_cache))
        def _():
            step(ck_ref, cv_ref)

        @pl.when(live & (b >= n_cache))
        def _():
            step(sk_ref, sv_ref)

        @pl.when(j == pl.num_programs(1) - 1)
        def _():
            denom = l_sc[...] + jnp.exp(sink_ref[...] - m_sc[...])
            o_ref[...] = (acc_sc[...] / denom).astype(o_ref.dtype)

    def cache_k(p, j, s):
        return (jnp.minimum(block_of(j, s), n_cache - 1), p)

    def cache_v(p, j, s):
        return (jnp.minimum(block_of(j, s), n_cache - 1), v_off + p)

    def stretch_k(p, j, s):
        return (jnp.maximum(block_of(j, s) - n_cache, 0), p)

    def stretch_v(p, j, s):
        return (jnp.maximum(block_of(j, s) - n_cache, 0), v_off + p)

    grid_spec = pltpu.PrefetchScalarGridSpec(
        num_scalar_prefetch=1,
        grid=(pairs, n_blocks),
        in_specs=[
            pl.BlockSpec((None, rows, lanes), lambda p, j, s: (p, 0, 0)),
            pl.BlockSpec((rows, 1), lambda p, j, s: (0, 0)),
            pl.BlockSpec((rows, 1), lambda p, j, s: (0, 0)),
            pl.BlockSpec((None, rows, 1), lambda p, j, s: (p, 0, 0)),
            pl.BlockSpec((TK, lanes), cache_k),
            pl.BlockSpec((TK, lanes), cache_v),
            pl.BlockSpec((TK, lanes), stretch_k),
            pl.BlockSpec((TK, lanes), stretch_v),
        ],
        out_specs=pl.BlockSpec((None, rows, lanes), lambda p, j, s: (p, 0, 0)),
        scratch_shapes=[
            pltpu.VMEM((rows, 1), jnp.float32),
            pltpu.VMEM((rows, 1), jnp.float32),
            pltpu.VMEM((rows, lanes), jnp.float32),
        ],
    )
    flops = 4 * pairs * rows * lanes * TK * n_blocks
    return pl.pallas_call(
        kernel,
        grid_spec=grid_spec,
        out_shape=jax.ShapeDtypeStruct((pairs, rows, lanes), jnp.bfloat16),
        compiler_params=pltpu.CompilerParams(dimension_semantics=("arbitrary", "arbitrary")),
        cost_estimate=pl.CostEstimate(
            flops=flops // 2,
            transcendentals=pairs * rows * TK * n_blocks // 2,
            bytes_accessed=2 * (cache_g.size + stretch_g.size) + 4 * qpad.size,
        ),
    )(bounds, qpad, qpos, qstart, sink_rows, cache_g, cache_g, stretch_g, stretch_g)


def attention(queries_local, cache_g, stretch_g, sinks, query_pos, query_start):
    tokens = queries_local.shape[0]
    groups = HEADS // KVH
    pairs = KVH // 2
    q6 = queries_local.reshape(tokens, pairs, 2, groups, HD).transpose(1, 2, 3, 0, 4)
    zeros = jnp.zeros_like(q6[:, 0])
    qpad = jnp.stack(
        [jnp.concatenate([q6[:, 0], zeros], axis=-1), jnp.concatenate([zeros, q6[:, 1]], axis=-1)], axis=1
    ).reshape(pairs, 2 * groups * tokens, 2 * HD)
    rows = 2 * groups * tokens
    qpos = jnp.tile(query_pos, 2 * groups).reshape(rows, 1)
    qstart = jnp.tile(query_start, 2 * groups).reshape(rows, 1)
    sink_rows = jnp.repeat(sinks.reshape(pairs, 2 * groups), tokens, axis=1).reshape(pairs, rows, 1)
    bounds = jnp.stack([query_start[0] // TK, query_pos[-1] // TK]).astype(jnp.int32)
    out = flash_pairs(qpad, qpos, qstart, sink_rows, cache_g, stretch_g, bounds, 1.0 / math.sqrt(HD))
    o6 = out.reshape(pairs, 2, groups, tokens, 2, HD)
    picked = jnp.stack([o6[:, 0, :, :, 0], o6[:, 1, :, :, 1]], axis=1)
    return picked.transpose(3, 0, 1, 2, 4).reshape(tokens, HEADS * HD)


def doc_index(positions, lengths):
    ends = jnp.cumsum(lengths)
    return jnp.sum((positions[:, None] >= ends[None, :]).astype(jnp.int32), axis=1)


def gated_act(pre, half_width):
    gate = pre[:, :half_width]
    upper = pre[:, half_width:]
    return ((upper + 1.0) * gate * jax.nn.sigmoid(1.702 * gate)).astype(jnp.bfloat16)


def body(
    residual,
    queries,
    stretch_kv,
    cache_kv,
    doc_lengths,
    sinks,
    out_proj,
    norm_gain,
    router,
    expert_ids,
    expert_in,
    expert_out,
):
    tokens = residual.shape[1]
    width = residual.shape[2]
    cache_rows = cache_kv.shape[1]
    kv_cols = stretch_kv.shape[2] // 2
    groups = HEADS // KVH
    ctx_count = lax.axis_size("ctx")
    ctx_here = lax.axis_index("ctx")
    stretch_base = cache_rows * ctx_count
    span = cache_rows + tokens
    query_pos = stretch_base + ctx_here * tokens + jnp.arange(tokens, dtype=jnp.int32)
    lengths = doc_lengths[0]
    ends = jnp.cumsum(lengths)
    query_start = jnp.max(
        jnp.where(ends[None, :] <= query_pos[:, None], ends[None, :], 0), axis=1
    ).astype(jnp.int32)
    cache_all = lax.all_gather(cache_kv[0], "ctx", axis=0, tiled=True)
    stretch_all = lax.all_gather(stretch_kv[0], "ctx", axis=0, tiled=True)
    attended = attention(queries[0], cache_all, stretch_all, sinks, query_pos, query_start)
    grp_here = lax.axis_index("grp")
    parity = grp_here % 2
    grp_count = lax.axis_size("grp")
    pair_perm = [(g, g ^ 1) for g in range(grp_count)]
    head_rows = out_proj.shape[0] // 2
    proj_half = lax.all_gather(
        lax.dynamic_slice_in_dim(out_proj, parity * head_rows, head_rows, 0), "ctx", axis=0, tiled=True
    )
    by_parity = attended.reshape(tokens, HEADS // 2, 2, HD)
    mine = jnp.where(parity == 0, by_parity[:, :, 0], by_parity[:, :, 1]).reshape(tokens, -1)
    theirs_cols = jnp.where(parity == 0, by_parity[:, :, 1], by_parity[:, :, 0]).reshape(tokens, -1)
    partner_cols = lax.ppermute(theirs_cols, "grp", pair_perm)
    both = jnp.dot(
        jnp.concatenate([mine, partner_cols], axis=0), proj_half, preferred_element_type=jnp.float32
    )
    back = lax.ppermute(both[tokens:], "grp", pair_perm)
    projected = both[:tokens] + back
    mid = (residual[0].astype(jnp.float32) + projected).astype(jnp.bfloat16)
    mid_float = mid.astype(jnp.float32)
    normed = (
        mid_float
        * lax.rsqrt(jnp.mean(mid_float * mid_float, axis=-1, keepdims=True) + 1e-05)
        * norm_gain
    ).astype(jnp.bfloat16)
    logits = jnp.dot(normed, router, preferred_element_type=jnp.float32)
    experts = router.shape[1]
    chosen_ids = expert_ids[0]
    topk = chosen_ids.shape[1]
    picks = chosen_ids[:, :, None] == jnp.arange(experts, dtype=jnp.int32)[None, None, :]
    chosen = jnp.sum(jnp.where(picks, logits[:, None, :], 0.0), axis=-1)
    raised = jnp.exp(chosen)
    route_weights = raised / jnp.sum(raised, axis=-1, keepdims=True)
    capacity = 2 * ((5 * tokens * topk + 8 * experts - 1) // (8 * experts))
    flat_ids = chosen_ids.reshape(-1)
    pairs = flat_ids.shape[0]
    onehot = (flat_ids[:, None] == jnp.arange(experts, dtype=jnp.int32)[None, :]).astype(jnp.int32)
    slots = jnp.sum(onehot * (jnp.cumsum(onehot, axis=0) - 1), axis=1)
    dest = flat_ids * capacity + slots
    source_rows = jnp.arange(pairs, dtype=jnp.int32) // topk
    packed = jnp.zeros((experts * capacity, width), jnp.bfloat16).at[dest].set(normed[source_rows])
    packed = packed.reshape(experts, capacity, width)
    in_weights = expert_in[0]
    out_weights = expert_out[0]
    half_width = out_weights.shape[0]
    owners = 2 * experts
    half_cap = capacity // 2
    split = packed.reshape(owners, half_cap, width)
    received = lax.all_to_all(split, ("ctx", "grp"), split_axis=0, concat_axis=0, tiled=True)
    partner_rows = lax.ppermute(received, "grp", pair_perm)

    def expert_half(rows):
        pre = jnp.dot(rows.reshape(-1, width), in_weights, preferred_element_type=jnp.float32)
        hidden = gated_act(pre, half_width)
        return jnp.dot(hidden, out_weights, preferred_element_type=jnp.float32).astype(jnp.bfloat16)

    own_part = expert_half(received)
    partner_part = expert_half(partner_rows)
    partner_back = lax.ppermute(partner_part, "grp", pair_perm)
    summed = (own_part.astype(jnp.float32) + partner_back.astype(jnp.float32)).astype(jnp.bfloat16)
    returned = lax.all_to_all(
        summed.reshape(owners, half_cap, width), ("ctx", "grp"), split_axis=0, concat_axis=0, tiled=True
    )
    expert_rows = returned.reshape(experts * capacity, width)
    gathered = expert_rows[dest].astype(jnp.float32) * route_weights.reshape(-1)[:, None]
    mixture = jnp.sum(gathered.reshape(tokens, topk, width), axis=1)
    final = (mid_float + mixture).astype(jnp.bfloat16)
    return (mid[None], final[None])


def solution(mesh):
    return jax.shard_map(
        body,
        mesh=mesh,
        in_specs=(
            P("grp", "ctx", None),
            P("grp", "ctx", None),
            P("grp", "ctx", None),
            P("grp", "ctx", None),
            P("grp", None),
            P(),
            P("ctx", None),
            P(),
            P(),
            P("grp", "ctx", None),
            P(("ctx", "grp"), None, None),
            P(("ctx", "grp"), None, None),
        ),
        out_specs=(P("grp", "ctx", None), P("grp", "ctx", None)),
        check_vma=False,
    )
```

```python
import math

import jax
import jax.numpy as jnp
from jax import lax
from jax.experimental import pallas as pl
from jax.experimental.pallas import tpu as pltpu
from jax.sharding import PartitionSpec as P

HEADS = 32
KVH = 8
HD = 64
TK = 512


def flash_pairs(qpad, qpos, qstart, sink_rows, cache_g, stretch_g, bounds, scale):
    pairs, rows, lanes = qpad.shape
    n_cache = cache_g.shape[0] // TK
    n_blocks = n_cache + stretch_g.shape[0] // TK
    v_off = cache_g.shape[1] // lanes // 2

    def block_of(j, s):
        return jnp.minimum(s[0] + j, s[1])

    def kernel(s_ref, q_ref, qpos_ref, qstart_ref, sink_ref, ck_ref, cv_ref, sk_ref, sv_ref, o_ref, m_sc, l_sc, acc_sc):
        j = pl.program_id(1)
        b = s_ref[0] + j

        @pl.when(j == 0)
        def _():
            m_sc[...] = sink_ref[...]
            l_sc[...] = jnp.zeros_like(l_sc)
            acc_sc[...] = jnp.zeros_like(acc_sc)

        def step(k_ref, v_ref):
            s = lax.dot_general(
                q_ref[...], k_ref[...], (((1,), (1,)), ((), ())), preferred_element_type=jnp.float32
            ) * scale
            kpos = b * TK + lax.broadcasted_iota(jnp.int32, (1, TK), 1)
            allowed = (kpos <= qpos_ref[...]) & (kpos >= qstart_ref[...])
            m_prev = m_sc[...]
            m_new = jnp.maximum(m_prev, jnp.max(jnp.where(allowed, s, -jnp.inf), axis=1, keepdims=True))
            p = jnp.where(allowed, jnp.exp(s - m_new), 0.0)
            shrink = jnp.exp(m_prev - m_new)
            l_sc[...] = l_sc[...] * shrink + jnp.sum(p, axis=1, keepdims=True)
            acc_sc[...] = acc_sc[...] * shrink + jnp.dot(
                p.astype(jnp.bfloat16), v_ref[...], preferred_element_type=jnp.float32
            )
            m_sc[...] = m_new

        live = b <= s_ref[1]

        @pl.when(live & (b < n_cache))
        def _():
            step(ck_ref, cv_ref)

        @pl.when(live & (b >= n_cache))
        def _():
            step(sk_ref, sv_ref)

        @pl.when(j == pl.num_programs(1) - 1)
        def _():
            denom = l_sc[...] + jnp.exp(sink_ref[...] - m_sc[...])
            o_ref[...] = (acc_sc[...] / denom).astype(o_ref.dtype)

    def cache_k(p, j, s):
        return (jnp.minimum(block_of(j, s), n_cache - 1), p)

    def cache_v(p, j, s):
        return (jnp.minimum(block_of(j, s), n_cache - 1), v_off + p)

    def stretch_k(p, j, s):
        return (jnp.maximum(block_of(j, s) - n_cache, 0), p)

    def stretch_v(p, j, s):
        return (jnp.maximum(block_of(j, s) - n_cache, 0), v_off + p)

    grid_spec = pltpu.PrefetchScalarGridSpec(
        num_scalar_prefetch=1,
        grid=(pairs, n_blocks),
        in_specs=[
            pl.BlockSpec((None, rows, lanes), lambda p, j, s: (p, 0, 0)),
            pl.BlockSpec((rows, 1), lambda p, j, s: (0, 0)),
            pl.BlockSpec((rows, 1), lambda p, j, s: (0, 0)),
            pl.BlockSpec((None, rows, 1), lambda p, j, s: (p, 0, 0)),
            pl.BlockSpec((TK, lanes), cache_k),
            pl.BlockSpec((TK, lanes), cache_v),
            pl.BlockSpec((TK, lanes), stretch_k),
            pl.BlockSpec((TK, lanes), stretch_v),
        ],
        out_specs=pl.BlockSpec((None, rows, lanes), lambda p, j, s: (p, 0, 0)),
        scratch_shapes=[
            pltpu.VMEM((rows, 1), jnp.float32),
            pltpu.VMEM((rows, 1), jnp.float32),
            pltpu.VMEM((rows, lanes), jnp.float32),
        ],
    )
    flops = 4 * pairs * rows * lanes * TK * n_blocks
    return pl.pallas_call(
        kernel,
        grid_spec=grid_spec,
        out_shape=jax.ShapeDtypeStruct((pairs, rows, lanes), jnp.bfloat16),
        compiler_params=pltpu.CompilerParams(dimension_semantics=("arbitrary", "arbitrary")),
        cost_estimate=pl.CostEstimate(
            flops=flops // 2,
            transcendentals=pairs * rows * TK * n_blocks // 2,
            bytes_accessed=2 * (cache_g.size + stretch_g.size) + 4 * qpad.size,
        ),
    )(bounds, qpad, qpos, qstart, sink_rows, cache_g, cache_g, stretch_g, stretch_g)


def attention(queries_local, cache_g, stretch_g, sinks, query_pos, query_start):
    tokens = queries_local.shape[0]
    groups = HEADS // KVH
    pairs = KVH // 2
    q6 = queries_local.reshape(tokens, pairs, 2, groups, HD).transpose(1, 2, 3, 0, 4)
    zeros = jnp.zeros_like(q6[:, 0])
    qpad = jnp.stack(
        [jnp.concatenate([q6[:, 0], zeros], axis=-1), jnp.concatenate([zeros, q6[:, 1]], axis=-1)], axis=1
    ).reshape(pairs, 2 * groups * tokens, 2 * HD)
    rows = 2 * groups * tokens
    qpos = jnp.tile(query_pos, 2 * groups).reshape(rows, 1)
    qstart = jnp.tile(query_start, 2 * groups).reshape(rows, 1)
    sink_rows = jnp.repeat(sinks.reshape(pairs, 2 * groups), tokens, axis=1).reshape(pairs, rows, 1)
    bounds = jnp.stack([query_start[0] // TK, query_pos[-1] // TK]).astype(jnp.int32)
    out = flash_pairs(qpad, qpos, qstart, sink_rows, cache_g, stretch_g, bounds, 1.0 / math.sqrt(HD))
    o6 = out.reshape(pairs, 2, groups, tokens, 2, HD)
    picked = jnp.stack([o6[:, 0, :, :, 0], o6[:, 1, :, :, 1]], axis=1)
    return picked.transpose(3, 0, 1, 2, 4).reshape(tokens, HEADS * HD)


def doc_index(positions, lengths):
    ends = jnp.cumsum(lengths)
    return jnp.sum((positions[:, None] >= ends[None, :]).astype(jnp.int32), axis=1)


def gated_act(pre, half_width):
    gate = pre[:, :half_width]
    upper = pre[:, half_width:]
    return ((upper + 1.0) * gate * jax.nn.sigmoid(1.702 * gate)).astype(jnp.bfloat16)


def body(
    residual,
    queries,
    stretch_kv,
    cache_kv,
    doc_lengths,
    sinks,
    out_proj,
    norm_gain,
    router,
    expert_ids,
    expert_in,
    expert_out,
):
    tokens = residual.shape[1]
    width = residual.shape[2]
    cache_rows = cache_kv.shape[1]
    kv_cols = stretch_kv.shape[2] // 2
    groups = HEADS // KVH
    ctx_count = lax.axis_size("ctx")
    ctx_here = lax.axis_index("ctx")
    stretch_base = cache_rows * ctx_count
    span = cache_rows + tokens
    query_pos = stretch_base + ctx_here * tokens + jnp.arange(tokens, dtype=jnp.int32)
    lengths = doc_lengths[0]
    ends = jnp.cumsum(lengths)
    query_start = jnp.max(
        jnp.where(ends[None, :] <= query_pos[:, None], ends[None, :], 0), axis=1
    ).astype(jnp.int32)
    cache_all = lax.all_gather(cache_kv[0], "ctx", axis=0, tiled=True)
    stretch_all = lax.all_gather(stretch_kv[0], "ctx", axis=0, tiled=True)
    attended = attention(queries[0], cache_all, stretch_all, sinks, query_pos, query_start)
    grp_here = lax.axis_index("grp")
    parity = grp_here % 2
    grp_count = lax.axis_size("grp")
    pair_perm = [(g, g ^ 1) for g in range(grp_count)]
    head_rows = out_proj.shape[0] // 2
    proj_half = lax.all_gather(
        lax.dynamic_slice_in_dim(out_proj, parity * head_rows, head_rows, 0), "ctx", axis=0, tiled=True
    )
    by_parity = attended.reshape(tokens, HEADS // 2, 2, HD)
    mine = jnp.where(parity == 0, by_parity[:, :, 0], by_parity[:, :, 1]).reshape(tokens, -1)
    theirs_cols = jnp.where(parity == 0, by_parity[:, :, 1], by_parity[:, :, 0]).reshape(tokens, -1)
    partner_cols = lax.ppermute(theirs_cols, "grp", pair_perm)
    both = jnp.dot(
        jnp.concatenate([mine, partner_cols], axis=0), proj_half, preferred_element_type=jnp.float32
    )
    back = lax.ppermute(both[tokens:], "grp", pair_perm)
    projected = both[:tokens] + back
    mid = (residual[0].astype(jnp.float32) + projected).astype(jnp.bfloat16)
    mid_float = mid.astype(jnp.float32)
    normed = (
        mid_float
        * lax.rsqrt(jnp.mean(mid_float * mid_float, axis=-1, keepdims=True) + 1e-05)
        * norm_gain
    ).astype(jnp.bfloat16)
    logits = jnp.dot(normed, router, preferred_element_type=jnp.float32)
    experts = router.shape[1]
    chosen_ids = expert_ids[0]
    topk = chosen_ids.shape[1]
    picks = chosen_ids[:, :, None] == jnp.arange(experts, dtype=jnp.int32)[None, None, :]
    chosen = jnp.sum(jnp.where(picks, logits[:, None, :], 0.0), axis=-1)
    raised = jnp.exp(chosen)
    route_weights = raised / jnp.sum(raised, axis=-1, keepdims=True)
    capacity = 2 * ((5 * tokens * topk + 8 * experts - 1) // (8 * experts))
    owners = 2 * experts
    half_cap = capacity // 2
    flat_ids = chosen_ids.reshape(-1)
    pairs = flat_ids.shape[0]
    onehot = (flat_ids[:, None] == jnp.arange(experts, dtype=jnp.int32)[None, :]).astype(jnp.int32)
    slots = jnp.sum(onehot * (jnp.cumsum(onehot, axis=0) - 1), axis=1)
    dest = (slots % half_cap) * owners + 2 * flat_ids + slots // half_cap
    source_rows = jnp.arange(pairs, dtype=jnp.int32) // topk
    slot_source = jnp.zeros((owners * half_cap,), jnp.int32).at[dest].set(source_rows)
    split = normed[slot_source].reshape(half_cap, owners, width)
    in_weights = expert_in[0]
    out_weights = expert_out[0]
    half_width = out_weights.shape[0]
    received = lax.all_to_all(split, ("ctx", "grp"), split_axis=1, concat_axis=1, tiled=True)
    partner_rows = lax.ppermute(received, "grp", pair_perm)

    def expert_half(rows):
        pre = jnp.dot(rows.reshape(-1, width), in_weights, preferred_element_type=jnp.float32)
        hidden = gated_act(pre, half_width)
        return jnp.dot(hidden, out_weights, preferred_element_type=jnp.float32).astype(jnp.bfloat16)

    own_part = expert_half(received)
    partner_part = expert_half(partner_rows)
    partner_back = lax.ppermute(partner_part, "grp", pair_perm)
    summed = (own_part.astype(jnp.float32) + partner_back.astype(jnp.float32)).astype(jnp.bfloat16)
    returned = lax.all_to_all(
        summed.reshape(half_cap, owners, width), ("ctx", "grp"), split_axis=1, concat_axis=1, tiled=True
    )
    expert_rows = returned.reshape(owners * half_cap, width)
    pair_dest = dest.reshape(tokens, topk)
    mixture = mid_float
    for k in range(topk):
        mixture = mixture + expert_rows[pair_dest[:, k]].astype(jnp.float32) * route_weights[:, k:k + 1]
    final = mixture.astype(jnp.bfloat16)
    return (mid[None], final[None])


def solution(mesh):
    return jax.shard_map(
        body,
        mesh=mesh,
        in_specs=(
            P("grp", "ctx", None),
            P("grp", "ctx", None),
            P("grp", "ctx", None),
            P("grp", "ctx", None),
            P("grp", None),
            P(),
            P("ctx", None),
            P(),
            P(),
            P("grp", "ctx", None),
            P(("ctx", "grp"), None, None),
            P(("ctx", "grp"), None, None),
        ),
        out_specs=(P("grp", "ctx", None), P("grp", "ctx", None)),
        check_vma=False,
    )
```

```python
import math

import jax
import jax.numpy as jnp
from jax import lax
from jax.experimental import pallas as pl
from jax.experimental.pallas import tpu as pltpu
from jax.sharding import PartitionSpec as P

HEADS = 32
KVH = 8
HD = 64
CACHE_TK = 256


def flash_pairs(qpad, qpos, qstart, sink_rows, kv_all, cache_rows, bounds, scale):
    pairs, rows, lanes = qpad.shape
    sources, span, width = kv_all.shape
    stretch_rows = span - cache_rows
    cache_steps = cache_rows // CACHE_TK
    n_cache = sources * cache_steps
    n_blocks = n_cache + sources
    v_off = width // lanes // 2

    def block_of(j, s):
        return jnp.minimum(s[0] + j, s[1])

    def kernel(s_ref, q_ref, qpos_ref, qstart_ref, sink_ref, ck_ref, cv_ref, sk_ref, sv_ref, o_ref, m_sc, l_sc, acc_sc):
        j = pl.program_id(1)
        b = s_ref[0] + j

        @pl.when(j == 0)
        def _():
            m_sc[...] = sink_ref[...]
            l_sc[...] = jnp.zeros_like(l_sc)
            acc_sc[...] = jnp.zeros_like(acc_sc)

        def step(k_ref, v_ref, first, count):
            s = lax.dot_general(
                q_ref[...], k_ref[...], (((1,), (1,)), ((), ())), preferred_element_type=jnp.float32
            ) * scale
            kpos = first + lax.broadcasted_iota(jnp.int32, (1, count), 1)
            allowed = (kpos <= qpos_ref[...]) & (kpos >= qstart_ref[...])
            m_prev = m_sc[...]
            m_new = jnp.maximum(m_prev, jnp.max(jnp.where(allowed, s, -jnp.inf), axis=1, keepdims=True))
            p = jnp.where(allowed, jnp.exp(s - m_new), 0.0)
            shrink = jnp.exp(m_prev - m_new)
            l_sc[...] = l_sc[...] * shrink + jnp.sum(p, axis=1, keepdims=True)
            acc_sc[...] = acc_sc[...] * shrink + jnp.dot(
                p.astype(jnp.bfloat16), v_ref[...], preferred_element_type=jnp.float32
            )
            m_sc[...] = m_new

        live = b <= s_ref[1]

        @pl.when(live & (b < n_cache))
        def _():
            step(ck_ref, cv_ref, b * CACHE_TK, CACHE_TK)

        @pl.when(live & (b >= n_cache))
        def _():
            step(sk_ref, sv_ref, sources * cache_rows + (b - n_cache) * stretch_rows, stretch_rows)

        @pl.when(j == pl.num_programs(1) - 1)
        def _():
            denom = l_sc[...] + jnp.exp(sink_ref[...] - m_sc[...])
            o_ref[...] = (acc_sc[...] / denom).astype(o_ref.dtype)

    def cache_at(j, s):
        c = jnp.minimum(block_of(j, s), n_cache - 1)
        return c // cache_steps, c % cache_steps

    def cache_k(p, j, s):
        src, part = cache_at(j, s)
        return (src, part, p)

    def cache_v(p, j, s):
        src, part = cache_at(j, s)
        return (src, part, v_off + p)

    def stretch_k(p, j, s):
        return (jnp.maximum(block_of(j, s) - n_cache, 0), cache_rows // stretch_rows, p)

    def stretch_v(p, j, s):
        return (jnp.maximum(block_of(j, s) - n_cache, 0), cache_rows // stretch_rows, v_off + p)

    grid_spec = pltpu.PrefetchScalarGridSpec(
        num_scalar_prefetch=1,
        grid=(pairs, n_blocks),
        in_specs=[
            pl.BlockSpec((None, rows, lanes), lambda p, j, s: (p, 0, 0)),
            pl.BlockSpec((rows, 1), lambda p, j, s: (0, 0)),
            pl.BlockSpec((rows, 1), lambda p, j, s: (0, 0)),
            pl.BlockSpec((None, rows, 1), lambda p, j, s: (p, 0, 0)),
            pl.BlockSpec((None, CACHE_TK, lanes), cache_k),
            pl.BlockSpec((None, CACHE_TK, lanes), cache_v),
            pl.BlockSpec((None, stretch_rows, lanes), stretch_k),
            pl.BlockSpec((None, stretch_rows, lanes), stretch_v),
        ],
        out_specs=pl.BlockSpec((None, rows, lanes), lambda p, j, s: (p, 0, 0)),
        scratch_shapes=[
            pltpu.VMEM((rows, 1), jnp.float32),
            pltpu.VMEM((rows, 1), jnp.float32),
            pltpu.VMEM((rows, lanes), jnp.float32),
        ],
    )
    keys = sources * span
    return pl.pallas_call(
        kernel,
        grid_spec=grid_spec,
        out_shape=jax.ShapeDtypeStruct((pairs, rows, lanes), jnp.bfloat16),
        compiler_params=pltpu.CompilerParams(dimension_semantics=("arbitrary", "arbitrary")),
        cost_estimate=pl.CostEstimate(
            flops=2 * pairs * rows * lanes * keys,
            transcendentals=pairs * rows * keys // 2,
            bytes_accessed=2 * kv_all.size + 4 * qpad.size,
        ),
    )(bounds, qpad, qpos, qstart, sink_rows, kv_all, kv_all, kv_all, kv_all)


def attention(queries_local, kv_all, cache_rows, sinks, query_pos, query_start):
    tokens = queries_local.shape[0]
    groups = HEADS // KVH
    pairs = KVH // 2
    sources, span, _ = kv_all.shape
    q6 = queries_local.reshape(tokens, pairs, 2, groups, HD).transpose(1, 2, 3, 0, 4)
    zeros = jnp.zeros_like(q6[:, 0])
    qpad = jnp.stack(
        [jnp.concatenate([q6[:, 0], zeros], axis=-1), jnp.concatenate([zeros, q6[:, 1]], axis=-1)], axis=1
    ).reshape(pairs, 2 * groups * tokens, 2 * HD)
    rows = 2 * groups * tokens
    qpos = jnp.tile(query_pos, 2 * groups).reshape(rows, 1)
    qstart = jnp.tile(query_start, 2 * groups).reshape(rows, 1)
    sink_rows = jnp.repeat(sinks.reshape(pairs, 2 * groups), tokens, axis=1).reshape(pairs, rows, 1)
    cache_end = sources * cache_rows
    stretch_rows = span - cache_rows
    low = query_start[0]
    first = jnp.where(
        low < cache_end, low // CACHE_TK, sources * (cache_rows // CACHE_TK) + (low - cache_end) // stretch_rows
    )
    last = sources * (cache_rows // CACHE_TK) + (query_pos[-1] - cache_end) // stretch_rows
    bounds = jnp.stack([first, last]).astype(jnp.int32)
    out = flash_pairs(qpad, qpos, qstart, sink_rows, kv_all, cache_rows, bounds, 1.0 / math.sqrt(HD))
    o6 = out.reshape(pairs, 2, groups, tokens, 2, HD)
    picked = jnp.stack([o6[:, 0, :, :, 0], o6[:, 1, :, :, 1]], axis=1)
    return picked.transpose(3, 0, 1, 2, 4).reshape(tokens, HEADS * HD)


def doc_index(positions, lengths):
    ends = jnp.cumsum(lengths)
    return jnp.sum((positions[:, None] >= ends[None, :]).astype(jnp.int32), axis=1)


def gated_act(pre, half_width):
    gate = pre[:, :half_width]
    upper = pre[:, half_width:]
    return ((upper + 1.0) * gate * jax.nn.sigmoid(1.702 * gate)).astype(jnp.bfloat16)


def body(
    residual,
    queries,
    stretch_kv,
    cache_kv,
    doc_lengths,
    sinks,
    out_proj,
    norm_gain,
    router,
    expert_ids,
    expert_in,
    expert_out,
):
    tokens = residual.shape[1]
    width = residual.shape[2]
    cache_rows = cache_kv.shape[1]
    kv_cols = stretch_kv.shape[2] // 2
    groups = HEADS // KVH
    ctx_count = lax.axis_size("ctx")
    ctx_here = lax.axis_index("ctx")
    stretch_base = cache_rows * ctx_count
    span = cache_rows + tokens
    query_pos = stretch_base + ctx_here * tokens + jnp.arange(tokens, dtype=jnp.int32)
    lengths = doc_lengths[0]
    ends = jnp.cumsum(lengths)
    query_start = jnp.max(
        jnp.where(ends[None, :] <= query_pos[:, None], ends[None, :], 0), axis=1
    ).astype(jnp.int32)
    local_kv = jnp.concatenate([cache_kv[0], stretch_kv[0]], axis=0)
    kv_all = lax.all_gather(local_kv, "ctx", axis=0, tiled=False)
    attended = attention(queries[0], kv_all, cache_rows, sinks, query_pos, query_start)
    grp_here = lax.axis_index("grp")
    parity = grp_here % 2
    grp_count = lax.axis_size("grp")
    pair_perm = [(g, g ^ 1) for g in range(grp_count)]
    head_rows = out_proj.shape[0] // 2
    proj_half = lax.all_gather(
        lax.dynamic_slice_in_dim(out_proj, parity * head_rows, head_rows, 0), "ctx", axis=0, tiled=True
    )
    by_parity = attended.reshape(tokens, HEADS // 2, 2, HD)
    mine = jnp.where(parity == 0, by_parity[:, :, 0], by_parity[:, :, 1]).reshape(tokens, -1)
    theirs_cols = jnp.where(parity == 0, by_parity[:, :, 1], by_parity[:, :, 0]).reshape(tokens, -1)
    partner_cols = lax.ppermute(theirs_cols, "grp", pair_perm)
    both = jnp.dot(
        jnp.concatenate([mine, partner_cols], axis=0), proj_half, preferred_element_type=jnp.float32
    )
    back = lax.ppermute(both[tokens:], "grp", pair_perm)
    projected = both[:tokens] + back
    mid = (residual[0].astype(jnp.float32) + projected).astype(jnp.bfloat16)
    mid_float = mid.astype(jnp.float32)
    normed = (
        mid_float
        * lax.rsqrt(jnp.mean(mid_float * mid_float, axis=-1, keepdims=True) + 1e-05)
        * norm_gain
    ).astype(jnp.bfloat16)
    logits = jnp.dot(normed, router, preferred_element_type=jnp.float32)
    experts = router.shape[1]
    chosen_ids = expert_ids[0]
    topk = chosen_ids.shape[1]
    picks = chosen_ids[:, :, None] == jnp.arange(experts, dtype=jnp.int32)[None, None, :]
    chosen = jnp.sum(jnp.where(picks, logits[:, None, :], 0.0), axis=-1)
    raised = jnp.exp(chosen)
    route_weights = raised / jnp.sum(raised, axis=-1, keepdims=True)
    capacity = 2 * ((5 * tokens * topk + 8 * experts - 1) // (8 * experts))
    owners = 2 * experts
    half_cap = capacity // 2
    flat_ids = chosen_ids.reshape(-1)
    pairs = flat_ids.shape[0]
    onehot = (flat_ids[:, None] == jnp.arange(experts, dtype=jnp.int32)[None, :]).astype(jnp.int32)
    slots = jnp.sum(onehot * (jnp.cumsum(onehot, axis=0) - 1), axis=1)
    dest = (slots % half_cap) * owners + 2 * flat_ids + slots // half_cap
    source_rows = jnp.arange(pairs, dtype=jnp.int32) // topk
    slot_source = jnp.zeros((owners * half_cap,), jnp.int32).at[dest].set(source_rows)
    split = normed[slot_source].reshape(half_cap, owners, width)
    in_weights = expert_in[0]
    out_weights = expert_out[0]
    half_width = out_weights.shape[0]
    received = lax.all_to_all(split, ("ctx", "grp"), split_axis=1, concat_axis=1, tiled=True)
    partner_rows = lax.ppermute(received, "grp", pair_perm)

    def expert_half(rows):
        pre = jnp.dot(rows.reshape(-1, width), in_weights, preferred_element_type=jnp.float32)
        hidden = gated_act(pre, half_width)
        return jnp.dot(hidden, out_weights, preferred_element_type=jnp.float32).astype(jnp.bfloat16)

    own_part = expert_half(received)
    partner_part = expert_half(partner_rows)
    partner_back = lax.ppermute(partner_part, "grp", pair_perm)
    summed = (own_part.astype(jnp.float32) + partner_back.astype(jnp.float32)).astype(jnp.bfloat16)
    returned = lax.all_to_all(
        summed.reshape(half_cap, owners, width), ("ctx", "grp"), split_axis=1, concat_axis=1, tiled=True
    )
    expert_rows = returned.reshape(owners * half_cap, width)
    pair_dest = dest.reshape(tokens, topk)
    mixture = mid_float
    for k in range(topk):
        mixture = mixture + expert_rows[pair_dest[:, k]].astype(jnp.float32) * route_weights[:, k:k + 1]
    final = mixture.astype(jnp.bfloat16)
    return (mid[None], final[None])


def solution(mesh):
    return jax.shard_map(
        body,
        mesh=mesh,
        in_specs=(
            P("grp", "ctx", None),
            P("grp", "ctx", None),
            P("grp", "ctx", None),
            P("grp", "ctx", None),
            P("grp", None),
            P(),
            P("ctx", None),
            P(),
            P(),
            P("grp", "ctx", None),
            P(("ctx", "grp"), None, None),
            P(("ctx", "grp"), None, None),
        ),
        out_specs=(P("grp", "ctx", None), P("grp", "ctx", None)),
        check_vma=False,
    )
```

```python
import math

import jax
import jax.numpy as jnp
from jax import lax
from jax.experimental import pallas as pl
from jax.experimental.pallas import tpu as pltpu
from jax.sharding import PartitionSpec as P

HEADS = 32
KVH = 8
HD = 64
CACHE_TK = 256


def flash_all(qpad, qpos, qstart, sink_rows, kv_all, cache_rows, bounds, steps, scale):
    pairs, rows, lanes = qpad.shape
    tokens = qpos.shape[0]
    sources, span, width = kv_all.shape
    stretch_rows = span - cache_rows
    cache_steps = cache_rows // CACHE_TK
    n_cache = sources * cache_steps
    v_base = width // 2
    reps = rows // tokens

    def block_of(j, s):
        return jnp.minimum(s[0] + j, s[1])

    def kernel(s_ref, q_ref, qpos_ref, qstart_ref, sink_ref, c_ref, t_ref, o_ref, m_sc, l_sc, acc_sc):
        j = pl.program_id(0)
        b = s_ref[0] + j

        @pl.when(j == 0)
        def _():
            m_sc[...] = sink_ref[...]
            l_sc[...] = jnp.zeros_like(l_sc)
            acc_sc[...] = jnp.zeros_like(acc_sc)

        def step(kv_ref, first, count, masked):
            if masked:
                kpos = first + lax.broadcasted_iota(jnp.int32, (1, count), 1)
                allowed = ((kpos <= qpos_ref[...]) & (kpos >= qstart_ref[...]))[None]
            for p in range(pairs):
                keys = kv_ref[:, p * lanes:(p + 1) * lanes]
                values = kv_ref[:, v_base + p * lanes:v_base + (p + 1) * lanes]
                s = lax.dot_general(
                    q_ref[p], keys, (((1,), (1,)), ((), ())), preferred_element_type=jnp.float32
                ) * scale
                m_prev = m_sc[p]
                if masked:
                    s3 = s.reshape(reps, tokens, count)
                    top = jnp.max(jnp.where(allowed, s3, -jnp.inf), axis=2, keepdims=True).reshape(rows, 1)
                    m_new = jnp.maximum(m_prev, top)
                    e3 = jnp.exp(s3 - m_new.reshape(reps, tokens, 1))
                    w = jnp.where(allowed, e3, 0.0).reshape(rows, count)
                else:
                    m_new = jnp.maximum(m_prev, jnp.max(s, axis=1, keepdims=True))
                    w = jnp.exp(s - m_new)
                shrink = jnp.exp(m_prev - m_new)
                l_sc[p] = l_sc[p] * shrink + jnp.sum(w, axis=1, keepdims=True)
                acc_sc[p] = acc_sc[p] * shrink + jnp.dot(
                    w.astype(jnp.bfloat16), values, preferred_element_type=jnp.float32
                )
                m_sc[p] = m_new

        live = b <= s_ref[1]

        def branch(kv_ref, first, count):
            inside = (first >= s_ref[3]) & (first + count - 1 <= s_ref[2])

            @pl.when(inside)
            def _():
                step(kv_ref, first, count, False)

            @pl.when(jnp.logical_not(inside))
            def _():
                step(kv_ref, first, count, True)

        @pl.when(live & (b < n_cache))
        def _():
            branch(c_ref, b * CACHE_TK, CACHE_TK)

        @pl.when(live & (b >= n_cache))
        def _():
            branch(t_ref, sources * cache_rows + (b - n_cache) * stretch_rows, stretch_rows)

        @pl.when(j == pl.num_programs(0) - 1)
        def _():
            denom = l_sc[...] + jnp.exp(sink_ref[...] - m_sc[...])
            o_ref[...] = (acc_sc[...] / denom).astype(o_ref.dtype)

    def cache_map(j, s):
        c = jnp.minimum(block_of(j, s), n_cache - 1)
        return (c // cache_steps, c % cache_steps, 0)

    def stretch_map(j, s):
        return (jnp.maximum(block_of(j, s) - n_cache, 0), cache_rows // stretch_rows, 0)

    grid_spec = pltpu.PrefetchScalarGridSpec(
        num_scalar_prefetch=1,
        grid=(steps,),
        in_specs=[
            pl.BlockSpec((pairs, rows, lanes), lambda j, s: (0, 0, 0)),
            pl.BlockSpec((tokens, 1), lambda j, s: (0, 0)),
            pl.BlockSpec((tokens, 1), lambda j, s: (0, 0)),
            pl.BlockSpec((pairs, rows, 1), lambda j, s: (0, 0, 0)),
            pl.BlockSpec((None, CACHE_TK, width), cache_map),
            pl.BlockSpec((None, stretch_rows, width), stretch_map),
        ],
        out_specs=pl.BlockSpec((pairs, rows, lanes), lambda j, s: (0, 0, 0)),
        scratch_shapes=[
            pltpu.VMEM((pairs, rows, 1), jnp.float32),
            pltpu.VMEM((pairs, rows, 1), jnp.float32),
            pltpu.VMEM((pairs, rows, lanes), jnp.float32),
        ],
    )
    keys = sources * span // 2
    return pl.pallas_call(
        kernel,
        grid_spec=grid_spec,
        out_shape=jax.ShapeDtypeStruct((pairs, rows, lanes), jnp.bfloat16),
        compiler_params=pltpu.CompilerParams(
            dimension_semantics=("arbitrary",), vmem_limit_bytes=48 * 1024 * 1024
        ),
        cost_estimate=pl.CostEstimate(
            flops=4 * pairs * rows * lanes * keys,
            transcendentals=pairs * rows * keys,
            bytes_accessed=kv_all.size + 4 * qpad.size,
        ),
    )(bounds, qpad, qpos, qstart, sink_rows, kv_all, kv_all)


def block_index(position, sources, cache_rows, stretch_rows):
    cache_end = sources * cache_rows
    return jnp.where(
        position < cache_end,
        position // CACHE_TK,
        sources * (cache_rows // CACHE_TK) + (position - cache_end) // stretch_rows,
    )


def attention(queries_local, kv_all, cache_rows, sinks, query_pos, query_start, longest):
    tokens = queries_local.shape[0]
    groups = HEADS // KVH
    pairs = KVH // 2
    sources, span, _ = kv_all.shape
    stretch_rows = span - cache_rows
    q6 = queries_local.reshape(tokens, pairs, 2, groups, HD).transpose(1, 2, 3, 0, 4)
    zeros = jnp.zeros_like(q6[:, 0])
    qpad = jnp.stack(
        [jnp.concatenate([q6[:, 0], zeros], axis=-1), jnp.concatenate([zeros, q6[:, 1]], axis=-1)], axis=1
    ).reshape(pairs, 2 * groups * tokens, 2 * HD)
    rows = 2 * groups * tokens
    sink_rows = jnp.repeat(sinks.reshape(pairs, 2 * groups), tokens, axis=1).reshape(pairs, rows, 1)
    first = block_index(query_start[0], sources, cache_rows, stretch_rows)
    last = block_index(query_pos[-1], sources, cache_rows, stretch_rows)
    bounds = jnp.stack([first, last, query_pos[0], query_start[-1]]).astype(jnp.int32)
    cache_end = sources * cache_rows

    def static_block(position):
        if position < cache_end:
            return position // CACHE_TK
        return sources * (cache_rows // CACHE_TK) + (position - cache_end) // stretch_rows

    steps = 1
    for device in range(sources):
        low_q = cache_end + device * tokens
        high_q = low_q + tokens - 1
        low = max(0, low_q - longest + 1)
        blocks = static_block(high_q) - static_block(low) + 1
        steps = max(steps, blocks)
    out = flash_all(
        qpad, query_pos.reshape(tokens, 1), query_start.reshape(tokens, 1), sink_rows, kv_all, cache_rows,
        bounds, steps, 1.0 / math.sqrt(HD),
    )
    o6 = out.reshape(pairs, 2, groups, tokens, 2, HD)
    picked = jnp.stack([o6[:, 0, :, :, 0], o6[:, 1, :, :, 1]], axis=1)
    return picked.transpose(3, 0, 1, 2, 4).reshape(tokens, HEADS * HD)


def doc_index(positions, lengths):
    ends = jnp.cumsum(lengths)
    return jnp.sum((positions[:, None] >= ends[None, :]).astype(jnp.int32), axis=1)


def gated_act(pre, half_width):
    gate = pre[:, :half_width]
    upper = pre[:, half_width:]
    return ((upper + 1.0) * gate * jax.nn.sigmoid(1.702 * gate)).astype(jnp.bfloat16)


def body(
    residual,
    queries,
    stretch_kv,
    cache_kv,
    doc_lengths,
    sinks,
    out_proj,
    norm_gain,
    router,
    expert_ids,
    expert_in,
    expert_out,
):
    tokens = residual.shape[1]
    width = residual.shape[2]
    cache_rows = cache_kv.shape[1]
    kv_cols = stretch_kv.shape[2] // 2
    groups = HEADS // KVH
    ctx_count = lax.axis_size("ctx")
    ctx_here = lax.axis_index("ctx")
    stretch_base = cache_rows * ctx_count
    span = cache_rows + tokens
    query_pos = stretch_base + ctx_here * tokens + jnp.arange(tokens, dtype=jnp.int32)
    lengths = doc_lengths[0]
    ends = jnp.cumsum(lengths)
    query_start = jnp.max(
        jnp.where(ends[None, :] <= query_pos[:, None], ends[None, :], 0), axis=1
    ).astype(jnp.int32)
    local_kv = jnp.concatenate([cache_kv[0], stretch_kv[0]], axis=0)
    kv_all = lax.all_gather(local_kv, "ctx", axis=0, tiled=False)
    attended = attention(queries[0], kv_all, cache_rows, sinks, query_pos, query_start, span * ctx_count // 2)
    grp_here = lax.axis_index("grp")
    parity = grp_here % 2
    grp_count = lax.axis_size("grp")
    pair_perm = [(g, g ^ 1) for g in range(grp_count)]
    head_rows = out_proj.shape[0] // 2
    proj_half = lax.all_gather(
        lax.dynamic_slice_in_dim(out_proj, parity * head_rows, head_rows, 0), "ctx", axis=0, tiled=True
    )
    by_parity = attended.reshape(tokens, HEADS // 2, 2, HD)
    mine = jnp.where(parity == 0, by_parity[:, :, 0], by_parity[:, :, 1]).reshape(tokens, -1)
    theirs_cols = jnp.where(parity == 0, by_parity[:, :, 1], by_parity[:, :, 0]).reshape(tokens, -1)
    partner_cols = lax.ppermute(theirs_cols, "grp", pair_perm)
    both = jnp.dot(
        jnp.concatenate([mine, partner_cols], axis=0), proj_half, preferred_element_type=jnp.float32
    )
    back = lax.ppermute(both[tokens:], "grp", pair_perm)
    projected = both[:tokens] + back
    mid = (residual[0].astype(jnp.float32) + projected).astype(jnp.bfloat16)
    mid_float = mid.astype(jnp.float32)
    normed = (
        mid_float
        * lax.rsqrt(jnp.mean(mid_float * mid_float, axis=-1, keepdims=True) + 1e-05)
        * norm_gain
    ).astype(jnp.bfloat16)
    logits = jnp.dot(normed, router, preferred_element_type=jnp.float32)
    experts = router.shape[1]
    chosen_ids = expert_ids[0]
    topk = chosen_ids.shape[1]
    picks = chosen_ids[:, :, None] == jnp.arange(experts, dtype=jnp.int32)[None, None, :]
    chosen = jnp.sum(jnp.where(picks, logits[:, None, :], 0.0), axis=-1)
    raised = jnp.exp(chosen)
    route_weights = raised / jnp.sum(raised, axis=-1, keepdims=True)
    capacity = 2 * ((5 * tokens * topk + 8 * experts - 1) // (8 * experts))
    owners = 2 * experts
    half_cap = capacity // 2
    flat_ids = chosen_ids.reshape(-1)
    pairs = flat_ids.shape[0]
    onehot = (flat_ids[:, None] == jnp.arange(experts, dtype=jnp.int32)[None, :]).astype(jnp.int32)
    slots = jnp.sum(onehot * (jnp.cumsum(onehot, axis=0) - 1), axis=1)
    dest = (slots % half_cap) * owners + 2 * flat_ids + slots // half_cap
    source_rows = jnp.arange(pairs, dtype=jnp.int32) // topk
    slot_source = jnp.zeros((owners * half_cap,), jnp.int32).at[dest].set(source_rows)
    split = normed[slot_source].reshape(half_cap, owners, width)
    in_weights = expert_in[0]
    out_weights = expert_out[0]
    half_width = out_weights.shape[0]
    received = lax.all_to_all(split, ("ctx", "grp"), split_axis=1, concat_axis=1, tiled=True)
    partner_rows = lax.ppermute(received, "grp", pair_perm)

    def expert_half(rows):
        pre = jnp.dot(rows.reshape(-1, width), in_weights, preferred_element_type=jnp.float32)
        hidden = gated_act(pre, half_width)
        return jnp.dot(hidden, out_weights, preferred_element_type=jnp.float32).astype(jnp.bfloat16)

    own_part = expert_half(received)
    partner_part = expert_half(partner_rows)
    partner_back = lax.ppermute(partner_part, "grp", pair_perm)
    summed = (own_part.astype(jnp.float32) + partner_back.astype(jnp.float32)).astype(jnp.bfloat16)
    returned = lax.all_to_all(
        summed.reshape(half_cap, owners, width), ("ctx", "grp"), split_axis=1, concat_axis=1, tiled=True
    )
    expert_rows = returned.reshape(owners * half_cap, width)
    pair_dest = dest.reshape(tokens, topk)
    mixture = mid_float
    for k in range(topk):
        mixture = mixture + expert_rows[pair_dest[:, k]].astype(jnp.float32) * route_weights[:, k:k + 1]
    final = mixture.astype(jnp.bfloat16)
    return (mid[None], final[None])


def solution(mesh):
    return jax.shard_map(
        body,
        mesh=mesh,
        in_specs=(
            P("grp", "ctx", None),
            P("grp", "ctx", None),
            P("grp", "ctx", None),
            P("grp", "ctx", None),
            P("grp", None),
            P(),
            P("ctx", None),
            P(),
            P(),
            P("grp", "ctx", None),
            P(("ctx", "grp"), None, None),
            P(("ctx", "grp"), None, None),
        ),
        out_specs=(P("grp", "ctx", None), P("grp", "ctx", None)),
        check_vma=False,
    )
```

```python
import math

import jax
import jax.numpy as jnp
from jax import lax
from jax.experimental import pallas as pl
from jax.experimental.pallas import tpu as pltpu
from jax.sharding import PartitionSpec as P

HEADS = 32
KVH = 8
HD = 64
CACHE_TK = 256


def flash_all(qpad, qpos, qstart, sink_rows, kv_all, cache_rows, bounds, steps, scale):
    pairs, rows, lanes = qpad.shape
    tokens = qpos.shape[0]
    sources, span, width = kv_all.shape
    stretch_rows = span - cache_rows
    cache_steps = cache_rows // CACHE_TK
    n_cache = sources * cache_steps
    v_base = width // 2
    reps = rows // tokens

    def block_of(j, s):
        return jnp.minimum(s[0] + j, s[1])

    def kernel(s_ref, q_ref, qpos_ref, qstart_ref, sink_ref, c_ref, t_ref, o_ref, m_sc, l_sc, acc_sc):
        j = pl.program_id(0)
        b = s_ref[0] + j

        @pl.when(j == 0)
        def _():
            m_sc[...] = sink_ref[...]
            l_sc[...] = jnp.zeros_like(l_sc)
            acc_sc[...] = jnp.zeros_like(acc_sc)

        def step(kv_ref, first, count, masked):
            if masked:
                kpos = first + lax.broadcasted_iota(jnp.int32, (1, count), 1)
                allowed = ((kpos <= qpos_ref[...]) & (kpos >= qstart_ref[...]))[None]
            for p in range(pairs):
                keys = kv_ref[:, p * lanes:(p + 1) * lanes]
                values = kv_ref[:, v_base + p * lanes:v_base + (p + 1) * lanes]
                s = lax.dot_general(
                    q_ref[p], keys, (((1,), (1,)), ((), ())), preferred_element_type=jnp.float32
                ) * scale
                m_prev = m_sc[p]
                if masked:
                    s3 = s.reshape(reps, tokens, count)
                    top = jnp.max(jnp.where(allowed, s3, -jnp.inf), axis=2, keepdims=True).reshape(rows, 1)
                    m_new = jnp.maximum(m_prev, top)
                    e3 = jnp.exp(s3 - m_new.reshape(reps, tokens, 1))
                    w = jnp.where(allowed, e3, 0.0).reshape(rows, count)
                else:
                    m_new = jnp.maximum(m_prev, jnp.max(s, axis=1, keepdims=True))
                    w = jnp.exp(s - m_new)
                shrink = jnp.exp(m_prev - m_new)
                l_sc[p] = l_sc[p] * shrink + jnp.sum(w, axis=1, keepdims=True)
                acc_sc[p] = acc_sc[p] * shrink + jnp.dot(
                    w.astype(jnp.bfloat16), values, preferred_element_type=jnp.float32
                )
                m_sc[p] = m_new

        live = b <= s_ref[1]

        def branch(kv_ref, first, count):
            inside = (first >= s_ref[3]) & (first + count - 1 <= s_ref[2])

            @pl.when(inside)
            def _():
                step(kv_ref, first, count, False)

            @pl.when(jnp.logical_not(inside))
            def _():
                step(kv_ref, first, count, True)

        @pl.when(live & (b < n_cache))
        def _():
            branch(c_ref, b * CACHE_TK, CACHE_TK)

        @pl.when(live & (b >= n_cache))
        def _():
            branch(t_ref, sources * cache_rows + (b - n_cache) * stretch_rows, stretch_rows)

        @pl.when(j == pl.num_programs(0) - 1)
        def _():
            denom = l_sc[...] + jnp.exp(sink_ref[...] - m_sc[...])
            o_ref[...] = (acc_sc[...] / denom).astype(o_ref.dtype)

    def cache_map(j, s):
        c = jnp.minimum(block_of(j, s), n_cache - 1)
        return (c // cache_steps, c % cache_steps, 0)

    def stretch_map(j, s):
        return (jnp.maximum(block_of(j, s) - n_cache, 0), cache_rows // stretch_rows, 0)

    grid_spec = pltpu.PrefetchScalarGridSpec(
        num_scalar_prefetch=1,
        grid=(steps,),
        in_specs=[
            pl.BlockSpec((pairs, rows, lanes), lambda j, s: (0, 0, 0)),
            pl.BlockSpec((tokens, 1), lambda j, s: (0, 0)),
            pl.BlockSpec((tokens, 1), lambda j, s: (0, 0)),
            pl.BlockSpec((pairs, rows, 1), lambda j, s: (0, 0, 0)),
            pl.BlockSpec((None, CACHE_TK, width), cache_map),
            pl.BlockSpec((None, stretch_rows, width), stretch_map),
        ],
        out_specs=pl.BlockSpec((pairs, rows, lanes), lambda j, s: (0, 0, 0)),
        scratch_shapes=[
            pltpu.VMEM((pairs, rows, 1), jnp.float32),
            pltpu.VMEM((pairs, rows, 1), jnp.float32),
            pltpu.VMEM((pairs, rows, lanes), jnp.float32),
        ],
    )
    keys = sources * span // 2
    return pl.pallas_call(
        kernel,
        grid_spec=grid_spec,
        out_shape=jax.ShapeDtypeStruct((pairs, rows, lanes), jnp.bfloat16),
        compiler_params=pltpu.CompilerParams(
            dimension_semantics=("arbitrary",), vmem_limit_bytes=48 * 1024 * 1024
        ),
        cost_estimate=pl.CostEstimate(
            flops=4 * pairs * rows * lanes * keys,
            transcendentals=pairs * rows * keys,
            bytes_accessed=kv_all.size + 4 * qpad.size,
        ),
    )(bounds, qpad, qpos, qstart, sink_rows, kv_all, kv_all)


def block_index(position, sources, cache_rows, stretch_rows):
    cache_end = sources * cache_rows
    return jnp.where(
        position < cache_end,
        position // CACHE_TK,
        sources * (cache_rows // CACHE_TK) + (position - cache_end) // stretch_rows,
    )


def attention(queries_local, kv_all, cache_rows, sinks, query_pos, query_start, longest):
    tokens = queries_local.shape[0]
    groups = HEADS // KVH
    pairs = KVH // 2
    sources, span, _ = kv_all.shape
    stretch_rows = span - cache_rows
    q6 = queries_local.reshape(tokens, pairs, 2, groups, HD).transpose(1, 2, 3, 0, 4)
    zeros = jnp.zeros_like(q6[:, 0])
    qpad = jnp.stack(
        [jnp.concatenate([q6[:, 0], zeros], axis=-1), jnp.concatenate([zeros, q6[:, 1]], axis=-1)], axis=1
    ).reshape(pairs, 2 * groups * tokens, 2 * HD)
    rows = 2 * groups * tokens
    sink_rows = jnp.repeat(sinks.reshape(pairs, 2 * groups), tokens, axis=1).reshape(pairs, rows, 1)
    first = block_index(query_start[0], sources, cache_rows, stretch_rows)
    last = block_index(query_pos[-1], sources, cache_rows, stretch_rows)
    bounds = jnp.stack([first, last, query_pos[0], query_start[-1]]).astype(jnp.int32)
    cache_end = sources * cache_rows

    def static_block(position):
        if position < cache_end:
            return position // CACHE_TK
        return sources * (cache_rows // CACHE_TK) + (position - cache_end) // stretch_rows

    steps = 1
    for device in range(sources):
        low_q = cache_end + device * tokens
        high_q = low_q + tokens - 1
        low = max(0, low_q - longest + 1)
        blocks = static_block(high_q) - static_block(low) + 1
        steps = max(steps, blocks)
    out = flash_all(
        qpad, query_pos.reshape(tokens, 1), query_start.reshape(tokens, 1), sink_rows, kv_all, cache_rows,
        bounds, steps, 1.0 / math.sqrt(HD),
    )
    o6 = out.reshape(pairs, 2, groups, tokens, 2, HD)
    picked = jnp.stack([o6[:, 0, :, :, 0], o6[:, 1, :, :, 1]], axis=1)
    return picked.transpose(3, 0, 1, 2, 4).reshape(tokens, HEADS * HD)


def doc_index(positions, lengths):
    ends = jnp.cumsum(lengths)
    return jnp.sum((positions[:, None] >= ends[None, :]).astype(jnp.int32), axis=1)


def gated_act(pre, half_width):
    gate = pre[:, :half_width]
    upper = pre[:, half_width:]
    return ((upper + 1.0) * gate * jax.nn.sigmoid(1.702 * gate)).astype(jnp.bfloat16)


def body(
    residual,
    queries,
    stretch_kv,
    cache_kv,
    doc_lengths,
    sinks,
    out_proj,
    norm_gain,
    router,
    expert_ids,
    expert_in,
    expert_out,
):
    tokens = residual.shape[1]
    width = residual.shape[2]
    cache_rows = cache_kv.shape[1]
    kv_cols = stretch_kv.shape[2] // 2
    groups = HEADS // KVH
    ctx_count = lax.axis_size("ctx")
    ctx_here = lax.axis_index("ctx")
    stretch_base = cache_rows * ctx_count
    span = cache_rows + tokens
    query_pos = stretch_base + ctx_here * tokens + jnp.arange(tokens, dtype=jnp.int32)
    lengths = doc_lengths[0]
    ends = jnp.cumsum(lengths)
    query_start = jnp.max(
        jnp.where(ends[None, :] <= query_pos[:, None], ends[None, :], 0), axis=1
    ).astype(jnp.int32)
    local_kv = jnp.concatenate([cache_kv[0], stretch_kv[0]], axis=0)
    kv_all = lax.all_gather(local_kv, "ctx", axis=0, tiled=False)
    attended = attention(queries[0], kv_all, cache_rows, sinks, query_pos, query_start, span * ctx_count // 2)
    grp_here = lax.axis_index("grp")
    parity = grp_here % 2
    grp_count = lax.axis_size("grp")
    pair_perm = [(g, g ^ 1) for g in range(grp_count)]
    head_rows = out_proj.shape[0] // 2
    proj_local = lax.dynamic_slice_in_dim(out_proj, parity * head_rows, head_rows, 0)
    proj_shards = [proj_local] + [
        lax.ppermute(proj_local, "ctx", [(s, (s + d) % ctx_count) for s in range(ctx_count)])
        for d in range(1, ctx_count)
    ]
    proj_half = jnp.stack(proj_shards).reshape(ctx_count * head_rows, -1)
    shard_order = (ctx_here - jnp.arange(ctx_count, dtype=jnp.int32)) % ctx_count
    by_parity = attended.reshape(tokens, HEADS // 2, 2, HD)
    mine = jnp.where(parity == 0, by_parity[:, :, 0], by_parity[:, :, 1]).reshape(tokens, -1)
    theirs_cols = jnp.where(parity == 0, by_parity[:, :, 1], by_parity[:, :, 0]).reshape(tokens, -1)
    partner_cols = lax.ppermute(theirs_cols, "grp", pair_perm)
    stacked = jnp.concatenate([mine, partner_cols], axis=0).reshape(2 * tokens, ctx_count, -1)
    both = jnp.dot(
        jnp.take(stacked, shard_order, axis=1).reshape(2 * tokens, -1), proj_half, preferred_element_type=jnp.float32
    )
    back = lax.ppermute(both[tokens:], "grp", pair_perm)
    projected = both[:tokens] + back
    mid = (residual[0].astype(jnp.float32) + projected).astype(jnp.bfloat16)
    mid_float = mid.astype(jnp.float32)
    normed = (
        mid_float
        * lax.rsqrt(jnp.mean(mid_float * mid_float, axis=-1, keepdims=True) + 1e-05)
        * norm_gain
    ).astype(jnp.bfloat16)
    logits = jnp.dot(normed, router, preferred_element_type=jnp.float32)
    experts = router.shape[1]
    chosen_ids = expert_ids[0]
    topk = chosen_ids.shape[1]
    picks = chosen_ids[:, :, None] == jnp.arange(experts, dtype=jnp.int32)[None, None, :]
    chosen = jnp.sum(jnp.where(picks, logits[:, None, :], 0.0), axis=-1)
    raised = jnp.exp(chosen)
    route_weights = raised / jnp.sum(raised, axis=-1, keepdims=True)
    capacity = 2 * ((5 * tokens * topk + 8 * experts - 1) // (8 * experts))
    owners = 2 * experts
    half_cap = capacity // 2
    flat_ids = chosen_ids.reshape(-1)
    pairs = flat_ids.shape[0]
    onehot = (flat_ids[:, None] == jnp.arange(experts, dtype=jnp.int32)[None, :]).astype(jnp.int32)
    slots = jnp.sum(onehot * (jnp.cumsum(onehot, axis=0) - 1), axis=1)
    dest = (slots % half_cap) * owners + 2 * flat_ids + slots // half_cap
    source_rows = jnp.arange(pairs, dtype=jnp.int32) // topk
    slot_source = jnp.zeros((owners * half_cap,), jnp.int32).at[dest].set(source_rows)
    split = normed[slot_source].reshape(half_cap, owners, width)
    in_weights = expert_in[0]
    out_weights = expert_out[0]
    half_width = out_weights.shape[0]
    received = lax.all_to_all(split, ("ctx", "grp"), split_axis=1, concat_axis=1, tiled=True)
    partner_rows = lax.ppermute(received, "grp", pair_perm)

    def expert_half(rows):
        pre = jnp.dot(rows.reshape(-1, width), in_weights, preferred_element_type=jnp.float32)
        hidden = gated_act(pre, half_width)
        return jnp.dot(hidden, out_weights, preferred_element_type=jnp.float32).astype(jnp.bfloat16)

    own_part = expert_half(received)
    partner_part = expert_half(partner_rows)
    partner_back = lax.ppermute(partner_part, "grp", pair_perm)
    summed = (own_part.astype(jnp.float32) + partner_back.astype(jnp.float32)).astype(jnp.bfloat16)
    returned = lax.all_to_all(
        summed.reshape(half_cap, owners, width), ("ctx", "grp"), split_axis=1, concat_axis=1, tiled=True
    )
    expert_rows = returned.reshape(owners * half_cap, width)
    pair_dest = dest.reshape(tokens, topk)
    mixture = mid_float
    for k in range(topk):
        mixture = mixture + expert_rows[pair_dest[:, k]].astype(jnp.float32) * route_weights[:, k:k + 1]
    final = mixture.astype(jnp.bfloat16)
    return (mid[None], final[None])


def solution(mesh):
    return jax.shard_map(
        body,
        mesh=mesh,
        in_specs=(
            P("grp", "ctx", None),
            P("grp", "ctx", None),
            P("grp", "ctx", None),
            P("grp", "ctx", None),
            P("grp", None),
            P(),
            P("ctx", None),
            P(),
            P(),
            P("grp", "ctx", None),
            P(("ctx", "grp"), None, None),
            P(("ctx", "grp"), None, None),
        ),
        out_specs=(P("grp", "ctx", None), P("grp", "ctx", None)),
        check_vma=False,
    )
```

```python
import math

import jax
import jax.numpy as jnp
from jax import lax
from jax.experimental import pallas as pl
from jax.experimental.pallas import tpu as pltpu
from jax.sharding import PartitionSpec as P

HEADS = 32
KVH = 8
HD = 64
CACHE_TK = 256


def flash_all(qpad, qpos, qstart, sink_rows, kv_all, cache_rows, bounds, steps, scale):
    pairs, rows, lanes = qpad.shape
    tokens = qpos.shape[0]
    sources, span, width = kv_all.shape
    stretch_rows = span - cache_rows
    cache_steps = cache_rows // CACHE_TK
    n_cache = sources * cache_steps
    v_base = width // 2
    reps = rows // tokens

    def block_of(j, s):
        return jnp.minimum(s[0] + j, s[1])

    def kernel(s_ref, q_ref, qpos_ref, qstart_ref, sink_ref, c_ref, t_ref, o_ref, m_sc, l_sc, acc_sc):
        j = pl.program_id(0)
        b = s_ref[0] + j

        @pl.when(j == 0)
        def _():
            m_sc[...] = sink_ref[...]
            l_sc[...] = jnp.zeros_like(l_sc)
            acc_sc[...] = jnp.zeros_like(acc_sc)

        def step(kv_ref, first, count, masked):
            if masked:
                kpos = first + lax.broadcasted_iota(jnp.int32, (1, count), 1)
                allowed = ((kpos <= qpos_ref[...]) & (kpos >= qstart_ref[...]))[None]
            for p in range(pairs):
                keys = kv_ref[:, p * lanes:(p + 1) * lanes]
                values = kv_ref[:, v_base + p * lanes:v_base + (p + 1) * lanes]
                s = lax.dot_general(
                    q_ref[p], keys, (((1,), (1,)), ((), ())), preferred_element_type=jnp.float32
                ) * scale
                m_prev = m_sc[p]
                if masked:
                    s3 = s.reshape(reps, tokens, count)
                    top = jnp.max(jnp.where(allowed, s3, -jnp.inf), axis=2, keepdims=True).reshape(rows, 1)
                    m_new = jnp.maximum(m_prev, top)
                    e3 = jnp.exp(s3 - m_new.reshape(reps, tokens, 1))
                    w = jnp.where(allowed, e3, 0.0).reshape(rows, count)
                else:
                    m_new = jnp.maximum(m_prev, jnp.max(s, axis=1, keepdims=True))
                    w = jnp.exp(s - m_new)
                shrink = jnp.exp(m_prev - m_new)
                l_sc[p] = l_sc[p] * shrink + jnp.sum(w, axis=1, keepdims=True)
                acc_sc[p] = acc_sc[p] * shrink + jnp.dot(
                    w.astype(jnp.bfloat16), values, preferred_element_type=jnp.float32
                )
                m_sc[p] = m_new

        live = b <= s_ref[1]

        def branch(kv_ref, first, count):
            inside = (first >= s_ref[3]) & (first + count - 1 <= s_ref[2])

            @pl.when(inside)
            def _():
                step(kv_ref, first, count, False)

            @pl.when(jnp.logical_not(inside))
            def _():
                step(kv_ref, first, count, True)

        @pl.when(live & (b < n_cache))
        def _():
            branch(c_ref, b * CACHE_TK, CACHE_TK)

        @pl.when(live & (b >= n_cache))
        def _():
            branch(t_ref, sources * cache_rows + (b - n_cache) * stretch_rows, stretch_rows)

        @pl.when(j == pl.num_programs(0) - 1)
        def _():
            denom = l_sc[...] + jnp.exp(sink_ref[...] - m_sc[...])
            o_ref[...] = (acc_sc[...] / denom).astype(o_ref.dtype)

    def cache_map(j, s):
        c = jnp.minimum(block_of(j, s), n_cache - 1)
        return (c // cache_steps, c % cache_steps, 0)

    def stretch_map(j, s):
        return (jnp.maximum(block_of(j, s) - n_cache, 0), cache_rows // stretch_rows, 0)

    grid_spec = pltpu.PrefetchScalarGridSpec(
        num_scalar_prefetch=1,
        grid=(steps,),
        in_specs=[
            pl.BlockSpec((pairs, rows, lanes), lambda j, s: (0, 0, 0)),
            pl.BlockSpec((tokens, 1), lambda j, s: (0, 0)),
            pl.BlockSpec((tokens, 1), lambda j, s: (0, 0)),
            pl.BlockSpec((pairs, rows, 1), lambda j, s: (0, 0, 0)),
            pl.BlockSpec((None, CACHE_TK, width), cache_map),
            pl.BlockSpec((None, stretch_rows, width), stretch_map),
        ],
        out_specs=pl.BlockSpec((pairs, rows, lanes), lambda j, s: (0, 0, 0)),
        scratch_shapes=[
            pltpu.VMEM((pairs, rows, 1), jnp.float32),
            pltpu.VMEM((pairs, rows, 1), jnp.float32),
            pltpu.VMEM((pairs, rows, lanes), jnp.float32),
        ],
    )
    keys = sources * span // 2
    return pl.pallas_call(
        kernel,
        grid_spec=grid_spec,
        out_shape=jax.ShapeDtypeStruct((pairs, rows, lanes), jnp.bfloat16),
        compiler_params=pltpu.CompilerParams(
            dimension_semantics=("arbitrary",), vmem_limit_bytes=48 * 1024 * 1024
        ),
        cost_estimate=pl.CostEstimate(
            flops=4 * pairs * rows * lanes * keys,
            transcendentals=pairs * rows * keys,
            bytes_accessed=kv_all.size + 4 * qpad.size,
        ),
    )(bounds, qpad, qpos, qstart, sink_rows, kv_all, kv_all)


def block_index(position, sources, cache_rows, stretch_rows):
    cache_end = sources * cache_rows
    return jnp.where(
        position < cache_end,
        position // CACHE_TK,
        sources * (cache_rows // CACHE_TK) + (position - cache_end) // stretch_rows,
    )


def attention(queries_local, kv_all, cache_rows, sinks, query_pos, query_start, longest):
    tokens = queries_local.shape[0]
    groups = HEADS // KVH
    pairs = KVH // 2
    sources, span, _ = kv_all.shape
    stretch_rows = span - cache_rows
    q6 = queries_local.reshape(tokens, pairs, 2, groups, HD).transpose(1, 2, 3, 0, 4)
    zeros = jnp.zeros_like(q6[:, 0])
    qpad = jnp.stack(
        [jnp.concatenate([q6[:, 0], zeros], axis=-1), jnp.concatenate([zeros, q6[:, 1]], axis=-1)], axis=1
    ).reshape(pairs, 2 * groups * tokens, 2 * HD)
    rows = 2 * groups * tokens
    sink_rows = jnp.repeat(sinks.reshape(pairs, 2 * groups), tokens, axis=1).reshape(pairs, rows, 1)
    first = block_index(query_start[0], sources, cache_rows, stretch_rows)
    last = block_index(query_pos[-1], sources, cache_rows, stretch_rows)
    bounds = jnp.stack([first, last, query_pos[0], query_start[-1]]).astype(jnp.int32)
    cache_end = sources * cache_rows

    def static_block(position):
        if position < cache_end:
            return position // CACHE_TK
        return sources * (cache_rows // CACHE_TK) + (position - cache_end) // stretch_rows

    steps = 1
    for device in range(sources):
        low_q = cache_end + device * tokens
        high_q = low_q + tokens - 1
        low = max(0, low_q - longest + 1)
        blocks = static_block(high_q) - static_block(low) + 1
        steps = max(steps, blocks)
    out = flash_all(
        qpad, query_pos.reshape(tokens, 1), query_start.reshape(tokens, 1), sink_rows, kv_all, cache_rows,
        bounds, steps, 1.0 / math.sqrt(HD),
    )
    o6 = out.reshape(pairs, 2, groups, tokens, 2, HD)
    picked = jnp.stack([o6[:, 0, :, :, 0], o6[:, 1, :, :, 1]], axis=1)
    return picked.transpose(3, 0, 1, 2, 4).reshape(tokens, HEADS * HD)


def doc_index(positions, lengths):
    ends = jnp.cumsum(lengths)
    return jnp.sum((positions[:, None] >= ends[None, :]).astype(jnp.int32), axis=1)


def gated_act(pre, half_width):
    gate = pre[:, :half_width]
    upper = pre[:, half_width:]
    return ((upper + 1.0) * gate * jax.nn.sigmoid(1.702 * gate)).astype(jnp.bfloat16)


def body(
    residual,
    queries,
    stretch_kv,
    cache_kv,
    doc_lengths,
    sinks,
    out_proj,
    norm_gain,
    router,
    expert_ids,
    expert_in,
    expert_out,
):
    tokens = residual.shape[1]
    width = residual.shape[2]
    cache_rows = cache_kv.shape[1]
    kv_cols = stretch_kv.shape[2] // 2
    groups = HEADS // KVH
    ctx_count = lax.axis_size("ctx")
    ctx_here = lax.axis_index("ctx")
    stretch_base = cache_rows * ctx_count
    span = cache_rows + tokens
    query_pos = stretch_base + ctx_here * tokens + jnp.arange(tokens, dtype=jnp.int32)
    lengths = doc_lengths[0]
    ends = jnp.cumsum(lengths)
    query_start = jnp.max(
        jnp.where(ends[None, :] <= query_pos[:, None], ends[None, :], 0), axis=1
    ).astype(jnp.int32)
    grp_here = lax.axis_index("grp")
    parity = grp_here % 2
    grp_count = lax.axis_size("grp")
    pair_perm = [(g, g ^ 1) for g in range(grp_count)]
    head_rows = out_proj.shape[0] // 2
    levels = grp_count // 2
    level = grp_here // 2
    sub_rows = head_rows // levels
    proj_piece = lax.all_gather(
        lax.dynamic_slice_in_dim(out_proj, parity * head_rows + level * sub_rows, sub_rows, 0), "ctx", axis=0
    )
    level_order = (level - jnp.arange(levels, dtype=jnp.int32)) % levels
    proj_piece, local_kv = lax.optimization_barrier(
        (proj_piece, jnp.concatenate([cache_kv[0], stretch_kv[0]], axis=0))
    )
    kv_all = lax.all_gather(local_kv, "ctx", axis=0, tiled=False)
    proj_half = jnp.stack(
        [proj_piece]
        + [
            lax.ppermute(proj_piece, "grp", [(g, (g + 2 * k) % grp_count) for g in range(grp_count)])
            for k in range(1, levels)
        ]
    ).reshape(ctx_count * head_rows, -1)
    attended = attention(queries[0], kv_all, cache_rows, sinks, query_pos, query_start, span * ctx_count // 2)
    by_parity = attended.reshape(tokens, HEADS // 2, 2, HD)
    mine = jnp.where(parity == 0, by_parity[:, :, 0], by_parity[:, :, 1]).reshape(tokens, -1)
    theirs_cols = jnp.where(parity == 0, by_parity[:, :, 1], by_parity[:, :, 0]).reshape(tokens, -1)
    partner_cols = lax.ppermute(theirs_cols, "grp", pair_perm)
    stacked = jnp.concatenate([mine, partner_cols], axis=0).reshape(2 * tokens, ctx_count, levels, sub_rows)
    stacked = jnp.take(stacked, level_order, axis=2).transpose(0, 2, 1, 3).reshape(2 * tokens, -1)
    both = jnp.dot(stacked, proj_half, preferred_element_type=jnp.float32)
    back = lax.ppermute(both[tokens:], "grp", pair_perm)
    projected = both[:tokens] + back
    mid = (residual[0].astype(jnp.float32) + projected).astype(jnp.bfloat16)
    mid_float = mid.astype(jnp.float32)
    normed = (
        mid_float
        * lax.rsqrt(jnp.mean(mid_float * mid_float, axis=-1, keepdims=True) + 1e-05)
        * norm_gain
    ).astype(jnp.bfloat16)
    logits = jnp.dot(normed, router, preferred_element_type=jnp.float32)
    experts = router.shape[1]
    chosen_ids = expert_ids[0]
    topk = chosen_ids.shape[1]
    picks = chosen_ids[:, :, None] == jnp.arange(experts, dtype=jnp.int32)[None, None, :]
    chosen = jnp.sum(jnp.where(picks, logits[:, None, :], 0.0), axis=-1)
    raised = jnp.exp(chosen)
    route_weights = raised / jnp.sum(raised, axis=-1, keepdims=True)
    capacity = 2 * ((5 * tokens * topk + 8 * experts - 1) // (8 * experts))
    owners = 2 * experts
    half_cap = capacity // 2
    flat_ids = chosen_ids.reshape(-1)
    pairs = flat_ids.shape[0]
    onehot = (flat_ids[:, None] == jnp.arange(experts, dtype=jnp.int32)[None, :]).astype(jnp.int32)
    slots = jnp.sum(onehot * (jnp.cumsum(onehot, axis=0) - 1), axis=1)
    dest = (slots % half_cap) * owners + 2 * flat_ids + slots // half_cap
    source_rows = jnp.arange(pairs, dtype=jnp.int32) // topk
    slot_source = jnp.zeros((owners * half_cap,), jnp.int32).at[dest].set(source_rows)
    split = normed[slot_source].reshape(half_cap, owners, width)
    in_weights = expert_in[0]
    out_weights = expert_out[0]
    half_width = out_weights.shape[0]
    received = lax.all_to_all(split, ("ctx", "grp"), split_axis=1, concat_axis=1, tiled=True)
    partner_rows = lax.ppermute(received, "grp", pair_perm)

    def expert_half(rows):
        pre = jnp.dot(rows.reshape(-1, width), in_weights, preferred_element_type=jnp.float32)
        hidden = gated_act(pre, half_width)
        return jnp.dot(hidden, out_weights, preferred_element_type=jnp.float32).astype(jnp.bfloat16)

    own_part = expert_half(received)
    partner_part = expert_half(partner_rows)
    partner_back = lax.ppermute(partner_part, "grp", pair_perm)
    summed = (own_part.astype(jnp.float32) + partner_back.astype(jnp.float32)).astype(jnp.bfloat16)
    returned = lax.all_to_all(
        summed.reshape(half_cap, owners, width), ("ctx", "grp"), split_axis=1, concat_axis=1, tiled=True
    )
    expert_rows = returned.reshape(owners * half_cap, width)
    pair_dest = dest.reshape(tokens, topk)
    mixture = mid_float
    for k in range(topk):
        mixture = mixture + expert_rows[pair_dest[:, k]].astype(jnp.float32) * route_weights[:, k:k + 1]
    final = mixture.astype(jnp.bfloat16)
    return (mid[None], final[None])


def solution(mesh):
    return jax.shard_map(
        body,
        mesh=mesh,
        in_specs=(
            P("grp", "ctx", None),
            P("grp", "ctx", None),
            P("grp", "ctx", None),
            P("grp", "ctx", None),
            P("grp", None),
            P(),
            P("ctx", None),
            P(),
            P(),
            P("grp", "ctx", None),
            P(("ctx", "grp"), None, None),
            P(("ctx", "grp"), None, None),
        ),
        out_specs=(P("grp", "ctx", None), P("grp", "ctx", None)),
        check_vma=False,
    )
```

```python
import math

import jax
import jax.numpy as jnp
from jax import lax
from jax.experimental import pallas as pl
from jax.experimental.pallas import tpu as pltpu
from jax.sharding import PartitionSpec as P

HEADS = 32
KVH = 8
HD = 64
CACHE_TK = 256


def flash_all(qpad, qpos, qstart, sink_rows, kv_all, cache_rows, bounds, steps, scale):
    pairs, rows, lanes = qpad.shape
    tokens = qpos.shape[0]
    sources, span, width = kv_all.shape
    stretch_rows = span - cache_rows
    cache_steps = cache_rows // CACHE_TK
    n_cache = sources * cache_steps
    v_base = width // 2
    reps = rows // tokens

    def block_of(j, s):
        return jnp.minimum(s[0] + j, s[1])

    def kernel(s_ref, q_ref, qpos_ref, qstart_ref, sink_ref, c_ref, t_ref, o_ref, m_sc, l_sc, acc_sc):
        j = pl.program_id(0)
        b = s_ref[0] + j

        @pl.when(j == 0)
        def _():
            m_sc[...] = sink_ref[...]
            l_sc[...] = jnp.zeros_like(l_sc)
            acc_sc[...] = jnp.zeros_like(acc_sc)

        def step(kv_ref, first, count, masked):
            if masked:
                kpos = first + lax.broadcasted_iota(jnp.int32, (1, count), 1)
                allowed = ((kpos <= qpos_ref[...]) & (kpos >= qstart_ref[...]))[None]
            for p in range(pairs):
                keys = kv_ref[:, p * lanes:(p + 1) * lanes]
                values = kv_ref[:, v_base + p * lanes:v_base + (p + 1) * lanes]
                s = lax.dot_general(
                    q_ref[p], keys, (((1,), (1,)), ((), ())), preferred_element_type=jnp.float32
                ) * scale
                m_prev = m_sc[p]
                if masked:
                    s3 = s.reshape(reps, tokens, count)
                    top = jnp.max(jnp.where(allowed, s3, -jnp.inf), axis=2, keepdims=True).reshape(rows, 1)
                    m_new = jnp.maximum(m_prev, top)
                    e3 = jnp.exp(s3 - m_new.reshape(reps, tokens, 1))
                    w = jnp.where(allowed, e3, 0.0).reshape(rows, count)
                else:
                    m_new = jnp.maximum(m_prev, jnp.max(s, axis=1, keepdims=True))
                    w = jnp.exp(s - m_new)
                shrink = jnp.exp(m_prev - m_new)
                l_sc[p] = l_sc[p] * shrink + jnp.sum(w, axis=1, keepdims=True)
                acc_sc[p] = acc_sc[p] * shrink + jnp.dot(
                    w.astype(jnp.bfloat16), values, preferred_element_type=jnp.float32
                )
                m_sc[p] = m_new

        live = b <= s_ref[1]

        def branch(kv_ref, first, count):
            inside = (first >= s_ref[3]) & (first + count - 1 <= s_ref[2])

            @pl.when(inside)
            def _():
                step(kv_ref, first, count, False)

            @pl.when(jnp.logical_not(inside))
            def _():
                step(kv_ref, first, count, True)

        @pl.when(live & (b < n_cache))
        def _():
            branch(c_ref, b * CACHE_TK, CACHE_TK)

        @pl.when(live & (b >= n_cache))
        def _():
            branch(t_ref, sources * cache_rows + (b - n_cache) * stretch_rows, stretch_rows)

        @pl.when(j == pl.num_programs(0) - 1)
        def _():
            denom = l_sc[...] + jnp.exp(sink_ref[...] - m_sc[...])
            o_ref[...] = (acc_sc[...] / denom).astype(o_ref.dtype)

    def cache_map(j, s):
        c = jnp.minimum(block_of(j, s), n_cache - 1)
        return (c // cache_steps, c % cache_steps, 0)

    def stretch_map(j, s):
        return (jnp.maximum(block_of(j, s) - n_cache, 0), cache_rows // stretch_rows, 0)

    grid_spec = pltpu.PrefetchScalarGridSpec(
        num_scalar_prefetch=1,
        grid=(steps,),
        in_specs=[
            pl.BlockSpec((pairs, rows, lanes), lambda j, s: (0, 0, 0)),
            pl.BlockSpec((tokens, 1), lambda j, s: (0, 0)),
            pl.BlockSpec((tokens, 1), lambda j, s: (0, 0)),
            pl.BlockSpec((pairs, rows, 1), lambda j, s: (0, 0, 0)),
            pl.BlockSpec((None, CACHE_TK, width), cache_map),
            pl.BlockSpec((None, stretch_rows, width), stretch_map),
        ],
        out_specs=pl.BlockSpec((pairs, rows, lanes), lambda j, s: (0, 0, 0)),
        scratch_shapes=[
            pltpu.VMEM((pairs, rows, 1), jnp.float32),
            pltpu.VMEM((pairs, rows, 1), jnp.float32),
            pltpu.VMEM((pairs, rows, lanes), jnp.float32),
        ],
    )
    keys = sources * span // 2
    return pl.pallas_call(
        kernel,
        grid_spec=grid_spec,
        out_shape=jax.ShapeDtypeStruct((pairs, rows, lanes), jnp.bfloat16),
        compiler_params=pltpu.CompilerParams(
            dimension_semantics=("arbitrary",), vmem_limit_bytes=48 * 1024 * 1024
        ),
        cost_estimate=pl.CostEstimate(
            flops=4 * pairs * rows * lanes * keys,
            transcendentals=pairs * rows * keys,
            bytes_accessed=kv_all.size + 4 * qpad.size,
        ),
    )(bounds, qpad, qpos, qstart, sink_rows, kv_all, kv_all)


def block_index(position, sources, cache_rows, stretch_rows):
    cache_end = sources * cache_rows
    return jnp.where(
        position < cache_end,
        position // CACHE_TK,
        sources * (cache_rows // CACHE_TK) + (position - cache_end) // stretch_rows,
    )


def attention(queries_local, kv_all, cache_rows, sinks, query_pos, query_start, longest):
    tokens = queries_local.shape[0]
    groups = HEADS // KVH
    pairs = KVH // 2
    sources, span, _ = kv_all.shape
    stretch_rows = span - cache_rows
    q6 = queries_local.reshape(tokens, pairs, 2, groups, HD).transpose(1, 2, 3, 0, 4)
    zeros = jnp.zeros_like(q6[:, 0])
    qpad = jnp.stack(
        [jnp.concatenate([q6[:, 0], zeros], axis=-1), jnp.concatenate([zeros, q6[:, 1]], axis=-1)], axis=1
    ).reshape(pairs, 2 * groups * tokens, 2 * HD)
    rows = 2 * groups * tokens
    sink_rows = jnp.repeat(sinks.reshape(pairs, 2 * groups), tokens, axis=1).reshape(pairs, rows, 1)
    first = block_index(query_start[0], sources, cache_rows, stretch_rows)
    last = block_index(query_pos[-1], sources, cache_rows, stretch_rows)
    bounds = jnp.stack([first, last, query_pos[0], query_start[-1]]).astype(jnp.int32)
    cache_end = sources * cache_rows

    def static_block(position):
        if position < cache_end:
            return position // CACHE_TK
        return sources * (cache_rows // CACHE_TK) + (position - cache_end) // stretch_rows

    steps = 1
    for device in range(sources):
        low_q = cache_end + device * tokens
        high_q = low_q + tokens - 1
        low = max(0, low_q - longest + 1)
        blocks = static_block(high_q) - static_block(low) + 1
        steps = max(steps, blocks)
    out = flash_all(
        qpad, query_pos.reshape(tokens, 1), query_start.reshape(tokens, 1), sink_rows, kv_all, cache_rows,
        bounds, steps, 1.0 / math.sqrt(HD),
    )
    o6 = out.reshape(pairs, 2, groups, tokens, 2, HD)
    picked = jnp.stack([o6[:, 0, :, :, 0], o6[:, 1, :, :, 1]], axis=1)
    return picked.transpose(3, 0, 1, 2, 4).reshape(tokens, HEADS * HD)


def doc_index(positions, lengths):
    ends = jnp.cumsum(lengths)
    return jnp.sum((positions[:, None] >= ends[None, :]).astype(jnp.int32), axis=1)


def gated_act(pre, half_width):
    gate = pre[:, :half_width]
    upper = pre[:, half_width:]
    return ((upper + 1.0) * gate * jax.nn.sigmoid(1.702 * gate)).astype(jnp.bfloat16)


def body(
    residual,
    queries,
    stretch_kv,
    cache_kv,
    doc_lengths,
    sinks,
    out_proj,
    norm_gain,
    router,
    expert_ids,
    expert_in,
    expert_out,
):
    tokens = residual.shape[1]
    width = residual.shape[2]
    cache_rows = cache_kv.shape[1]
    kv_cols = stretch_kv.shape[2] // 2
    groups = HEADS // KVH
    ctx_count = lax.axis_size("ctx")
    ctx_here = lax.axis_index("ctx")
    stretch_base = cache_rows * ctx_count
    span = cache_rows + tokens
    query_pos = stretch_base + ctx_here * tokens + jnp.arange(tokens, dtype=jnp.int32)
    lengths = doc_lengths[0]
    ends = jnp.cumsum(lengths)
    query_start = jnp.max(
        jnp.where(ends[None, :] <= query_pos[:, None], ends[None, :], 0), axis=1
    ).astype(jnp.int32)
    local_kv = jnp.concatenate([cache_kv[0], stretch_kv[0]], axis=0)
    kv_all = lax.all_gather(local_kv, "ctx", axis=0, tiled=False)
    attended = attention(queries[0], kv_all, cache_rows, sinks, query_pos, query_start, span * ctx_count // 2)
    grp_here = lax.axis_index("grp")
    parity = grp_here % 2
    grp_count = lax.axis_size("grp")
    pair_perm = [(g, g ^ 1) for g in range(grp_count)]
    head_rows = out_proj.shape[0] // 2
    proj_half = lax.all_gather(
        lax.dynamic_slice_in_dim(out_proj, parity * head_rows, head_rows, 0), "ctx", axis=0, tiled=True
    )
    by_parity = attended.reshape(tokens, HEADS // 2, 2, HD)
    mine = jnp.where(parity == 0, by_parity[:, :, 0], by_parity[:, :, 1]).reshape(tokens, -1)
    theirs_cols = jnp.where(parity == 0, by_parity[:, :, 1], by_parity[:, :, 0]).reshape(tokens, -1)
    partner_cols = lax.ppermute(theirs_cols, "grp", pair_perm)
    both = jnp.dot(
        jnp.concatenate([mine, partner_cols], axis=0), proj_half, preferred_element_type=jnp.float32
    )
    back = lax.ppermute(both[tokens:], "grp", pair_perm)
    projected = both[:tokens] + back
    mid = (residual[0].astype(jnp.float32) + projected).astype(jnp.bfloat16)
    mid_float = mid.astype(jnp.float32)
    normed = (
        mid_float
        * lax.rsqrt(jnp.mean(mid_float * mid_float, axis=-1, keepdims=True) + 1e-05)
        * norm_gain
    ).astype(jnp.bfloat16)
    logits = jnp.dot(normed, router, preferred_element_type=jnp.float32)
    experts = router.shape[1]
    chosen_ids = expert_ids[0]
    topk = chosen_ids.shape[1]
    picks = chosen_ids[:, :, None] == jnp.arange(experts, dtype=jnp.int32)[None, None, :]
    chosen = jnp.sum(jnp.where(picks, logits[:, None, :], 0.0), axis=-1)
    raised = jnp.exp(chosen)
    route_weights = raised / jnp.sum(raised, axis=-1, keepdims=True)
    capacity = 2 * ((5 * tokens * topk + 8 * experts - 1) // (8 * experts))
    owners = 2 * experts
    half_cap = capacity // 2
    flat_ids = chosen_ids.reshape(-1)
    pairs = flat_ids.shape[0]
    onehot = (flat_ids[:, None] == jnp.arange(experts, dtype=jnp.int32)[None, :]).astype(jnp.int32)
    slots = jnp.sum(onehot * (jnp.cumsum(onehot, axis=0) - 1), axis=1)
    dest = (slots % half_cap) * owners + 2 * flat_ids + slots // half_cap
    source_rows = jnp.arange(pairs, dtype=jnp.int32) // topk
    slot_source = jnp.zeros((owners * half_cap,), jnp.int32).at[dest].set(source_rows)
    split = normed[slot_source].reshape(half_cap, owners, width)
    in_weights = expert_in[0]
    out_weights = expert_out[0]
    half_width = out_weights.shape[0]
    received = lax.all_to_all(split, ("ctx", "grp"), split_axis=1, concat_axis=1, tiled=True)
    partner_rows = lax.ppermute(received, "grp", pair_perm)

    def expert_half(rows):
        pre = jnp.einsum("sow,wh->soh", rows, in_weights, preferred_element_type=jnp.float32)
        gate = pre[..., :half_width]
        upper = pre[..., half_width:]
        hidden = ((upper + 1.0) * gate * jax.nn.sigmoid(1.702 * gate)).astype(jnp.bfloat16)
        return jnp.einsum("soh,hw->sow", hidden, out_weights, preferred_element_type=jnp.float32).astype(
            jnp.bfloat16
        )

    own_part = expert_half(received)
    partner_part = expert_half(partner_rows)
    partner_back = lax.ppermute(partner_part, "grp", pair_perm)
    summed = (own_part.astype(jnp.float32) + partner_back.astype(jnp.float32)).astype(jnp.bfloat16)
    returned = lax.all_to_all(summed, ("ctx", "grp"), split_axis=1, concat_axis=1, tiled=True)
    order_dest = dest.reshape(tokens, topk).T.reshape(-1)
    picks = (order_dest[:, None] == jnp.arange(owners * half_cap, dtype=jnp.int32)[None, :]).astype(jnp.bfloat16)
    chosen_rows = jnp.einsum(
        "rso,sow->rw", picks.reshape(-1, half_cap, owners), returned, preferred_element_type=jnp.float32
    ).reshape(topk, tokens, width)
    mixture = mid_float
    for k in range(topk):
        mixture = mixture + chosen_rows[k] * route_weights[:, k:k + 1]
    final = mixture.astype(jnp.bfloat16)
    return (mid[None], final[None])


def solution(mesh):
    return jax.shard_map(
        body,
        mesh=mesh,
        in_specs=(
            P("grp", "ctx", None),
            P("grp", "ctx", None),
            P("grp", "ctx", None),
            P("grp", "ctx", None),
            P("grp", None),
            P(),
            P("ctx", None),
            P(),
            P(),
            P("grp", "ctx", None),
            P(("ctx", "grp"), None, None),
            P(("ctx", "grp"), None, None),
        ),
        out_specs=(P("grp", "ctx", None), P("grp", "ctx", None)),
        check_vma=False,
    )
```

```python
import math

import jax
import jax.numpy as jnp
from jax import lax
from jax.experimental import pallas as pl
from jax.experimental.pallas import tpu as pltpu
from jax.sharding import PartitionSpec as P

HEADS = 32
KVH = 8
HD = 64
CACHE_TK = 256


def flash_all(qpad, qpos, qstart, sink_rows, kv_all, cache_rows, bounds, steps, scale):
    pairs, rows, lanes = qpad.shape
    tokens = qpos.shape[0]
    sources, span, width = kv_all.shape
    stretch_rows = span - cache_rows
    cache_steps = cache_rows // CACHE_TK
    n_cache = sources * cache_steps
    v_base = width // 2
    reps = rows // tokens

    def block_of(j, s):
        return jnp.minimum(s[0] + j, s[1])

    def kernel(s_ref, q_ref, qpos_ref, qstart_ref, sink_ref, c_ref, t_ref, o_ref, m_sc, l_sc, acc_sc):
        j = pl.program_id(0)
        b = s_ref[0] + j

        @pl.when(j == 0)
        def _():
            m_sc[...] = sink_ref[...]
            l_sc[...] = jnp.zeros_like(l_sc)
            acc_sc[...] = jnp.zeros_like(acc_sc)

        def step(kv_ref, first, count, masked):
            if masked:
                kpos = first + lax.broadcasted_iota(jnp.int32, (1, count), 1)
                allowed = ((kpos <= qpos_ref[...]) & (kpos >= qstart_ref[...]))[None]
            for p in range(pairs):
                keys = kv_ref[:, p * lanes:(p + 1) * lanes]
                values = kv_ref[:, v_base + p * lanes:v_base + (p + 1) * lanes]
                s = lax.dot_general(
                    q_ref[p], keys, (((1,), (1,)), ((), ())), preferred_element_type=jnp.float32
                ) * scale
                m_prev = m_sc[p]
                if masked:
                    s3 = s.reshape(reps, tokens, count)
                    top = jnp.max(jnp.where(allowed, s3, -jnp.inf), axis=2, keepdims=True).reshape(rows, 1)
                    m_new = jnp.maximum(m_prev, top)
                    e3 = jnp.exp(s3 - m_new.reshape(reps, tokens, 1))
                    w = jnp.where(allowed, e3, 0.0).reshape(rows, count)
                else:
                    m_new = jnp.maximum(m_prev, jnp.max(s, axis=1, keepdims=True))
                    w = jnp.exp(s - m_new)
                shrink = jnp.exp(m_prev - m_new)
                l_sc[p] = l_sc[p] * shrink + jnp.sum(w, axis=1, keepdims=True)
                acc_sc[p] = acc_sc[p] * shrink + jnp.dot(
                    w.astype(jnp.bfloat16), values, preferred_element_type=jnp.float32
                )
                m_sc[p] = m_new

        live = b <= s_ref[1]

        def branch(kv_ref, first, count):
            inside = (first >= s_ref[3]) & (first + count - 1 <= s_ref[2])

            @pl.when(inside)
            def _():
                step(kv_ref, first, count, False)

            @pl.when(jnp.logical_not(inside))
            def _():
                step(kv_ref, first, count, True)

        @pl.when(live & (b < n_cache))
        def _():
            branch(c_ref, b * CACHE_TK, CACHE_TK)

        @pl.when(live & (b >= n_cache))
        def _():
            branch(t_ref, sources * cache_rows + (b - n_cache) * stretch_rows, stretch_rows)

        @pl.when(j == pl.num_programs(0) - 1)
        def _():
            denom = l_sc[...] + jnp.exp(sink_ref[...] - m_sc[...])
            o_ref[...] = (acc_sc[...] / denom).astype(o_ref.dtype)

    def cache_map(j, s):
        c = jnp.minimum(block_of(j, s), n_cache - 1)
        return (c // cache_steps, c % cache_steps, 0)

    def stretch_map(j, s):
        return (jnp.maximum(block_of(j, s) - n_cache, 0), cache_rows // stretch_rows, 0)

    grid_spec = pltpu.PrefetchScalarGridSpec(
        num_scalar_prefetch=1,
        grid=(steps,),
        in_specs=[
            pl.BlockSpec((pairs, rows, lanes), lambda j, s: (0, 0, 0)),
            pl.BlockSpec((tokens, 1), lambda j, s: (0, 0)),
            pl.BlockSpec((tokens, 1), lambda j, s: (0, 0)),
            pl.BlockSpec((pairs, rows, 1), lambda j, s: (0, 0, 0)),
            pl.BlockSpec((None, CACHE_TK, width), cache_map),
            pl.BlockSpec((None, stretch_rows, width), stretch_map),
        ],
        out_specs=pl.BlockSpec((pairs, rows, lanes), lambda j, s: (0, 0, 0)),
        scratch_shapes=[
            pltpu.VMEM((pairs, rows, 1), jnp.float32),
            pltpu.VMEM((pairs, rows, 1), jnp.float32),
            pltpu.VMEM((pairs, rows, lanes), jnp.float32),
        ],
    )
    keys = sources * span // 2
    return pl.pallas_call(
        kernel,
        grid_spec=grid_spec,
        out_shape=jax.ShapeDtypeStruct((pairs, rows, lanes), jnp.bfloat16),
        compiler_params=pltpu.CompilerParams(
            dimension_semantics=("arbitrary",), vmem_limit_bytes=48 * 1024 * 1024
        ),
        cost_estimate=pl.CostEstimate(
            flops=4 * pairs * rows * lanes * keys,
            transcendentals=pairs * rows * keys,
            bytes_accessed=kv_all.size + 4 * qpad.size,
        ),
    )(bounds, qpad, qpos, qstart, sink_rows, kv_all, kv_all)


def block_index(position, sources, cache_rows, stretch_rows):
    cache_end = sources * cache_rows
    return jnp.where(
        position < cache_end,
        position // CACHE_TK,
        sources * (cache_rows // CACHE_TK) + (position - cache_end) // stretch_rows,
    )


def attention(queries_local, kv_all, cache_rows, sinks, query_pos, query_start, longest):
    tokens = queries_local.shape[0]
    groups = HEADS // KVH
    pairs = KVH // 2
    sources, span, _ = kv_all.shape
    stretch_rows = span - cache_rows
    q6 = queries_local.reshape(tokens, pairs, 2, groups, HD).transpose(1, 2, 3, 0, 4)
    zeros = jnp.zeros_like(q6[:, 0])
    qpad = jnp.stack(
        [jnp.concatenate([q6[:, 0], zeros], axis=-1), jnp.concatenate([zeros, q6[:, 1]], axis=-1)], axis=1
    ).reshape(pairs, 2 * groups * tokens, 2 * HD)
    rows = 2 * groups * tokens
    sink_rows = jnp.repeat(sinks.reshape(pairs, 2 * groups), tokens, axis=1).reshape(pairs, rows, 1)
    first = block_index(query_start[0], sources, cache_rows, stretch_rows)
    last = block_index(query_pos[-1], sources, cache_rows, stretch_rows)
    bounds = jnp.stack([first, last, query_pos[0], query_start[-1]]).astype(jnp.int32)
    cache_end = sources * cache_rows

    def static_block(position):
        if position < cache_end:
            return position // CACHE_TK
        return sources * (cache_rows // CACHE_TK) + (position - cache_end) // stretch_rows

    steps = 1
    for device in range(sources):
        low_q = cache_end + device * tokens
        high_q = low_q + tokens - 1
        low = max(0, low_q - longest + 1)
        blocks = static_block(high_q) - static_block(low) + 1
        steps = max(steps, blocks)
    out = flash_all(
        qpad, query_pos.reshape(tokens, 1), query_start.reshape(tokens, 1), sink_rows, kv_all, cache_rows,
        bounds, steps, 1.0 / math.sqrt(HD),
    )
    o6 = out.reshape(pairs, 2, groups, tokens, 2, HD)
    picked = jnp.stack([o6[:, 0, :, :, 0], o6[:, 1, :, :, 1]], axis=1)
    return picked.transpose(3, 0, 1, 2, 4).reshape(tokens, HEADS * HD)


def doc_index(positions, lengths):
    ends = jnp.cumsum(lengths)
    return jnp.sum((positions[:, None] >= ends[None, :]).astype(jnp.int32), axis=1)


def gated_act(pre, half_width):
    gate = pre[:, :half_width]
    upper = pre[:, half_width:]
    return ((upper + 1.0) * gate * jax.nn.sigmoid(1.702 * gate)).astype(jnp.bfloat16)


def body(
    residual,
    queries,
    stretch_kv,
    cache_kv,
    doc_lengths,
    sinks,
    out_proj,
    norm_gain,
    router,
    expert_ids,
    expert_in,
    expert_out,
):
    tokens = residual.shape[1]
    width = residual.shape[2]
    cache_rows = cache_kv.shape[1]
    kv_cols = stretch_kv.shape[2] // 2
    groups = HEADS // KVH
    ctx_count = lax.axis_size("ctx")
    ctx_here = lax.axis_index("ctx")
    stretch_base = cache_rows * ctx_count
    span = cache_rows + tokens
    query_pos = stretch_base + ctx_here * tokens + jnp.arange(tokens, dtype=jnp.int32)
    lengths = doc_lengths[0]
    ends = jnp.cumsum(lengths)
    query_start = jnp.max(
        jnp.where(ends[None, :] <= query_pos[:, None], ends[None, :], 0), axis=1
    ).astype(jnp.int32)
    local_kv = jnp.concatenate([cache_kv[0], stretch_kv[0]], axis=0)
    kv_all = lax.all_gather(local_kv, "ctx", axis=0, tiled=False)
    attended = attention(queries[0], kv_all, cache_rows, sinks, query_pos, query_start, span * ctx_count // 2)
    grp_here = lax.axis_index("grp")
    parity = grp_here % 2
    grp_count = lax.axis_size("grp")
    pair_perm = [(g, g ^ 1) for g in range(grp_count)]
    head_rows = out_proj.shape[0] // 2
    proj_half = lax.all_gather(
        lax.dynamic_slice_in_dim(out_proj, parity * head_rows, head_rows, 0), "ctx", axis=0, tiled=True
    )
    by_parity = attended.reshape(tokens, HEADS // 2, 2, HD)
    mine = jnp.where(parity == 0, by_parity[:, :, 0], by_parity[:, :, 1]).reshape(tokens, -1)
    theirs_cols = jnp.where(parity == 0, by_parity[:, :, 1], by_parity[:, :, 0]).reshape(tokens, -1)
    partner_cols = lax.ppermute(theirs_cols, "grp", pair_perm)
    both = jnp.dot(
        jnp.concatenate([mine, partner_cols], axis=0), proj_half, preferred_element_type=jnp.float32
    )
    back = lax.ppermute(both[tokens:], "grp", pair_perm)
    projected = both[:tokens] + back
    mid = (residual[0].astype(jnp.float32) + projected).astype(jnp.bfloat16)
    mid_float = mid.astype(jnp.float32)
    normed = (
        mid_float
        * lax.rsqrt(jnp.mean(mid_float * mid_float, axis=-1, keepdims=True) + 1e-05)
        * norm_gain
    ).astype(jnp.bfloat16)
    logits = jnp.dot(normed, router, preferred_element_type=jnp.float32)
    experts = router.shape[1]
    chosen_ids = expert_ids[0]
    topk = chosen_ids.shape[1]
    picks = chosen_ids[:, :, None] == jnp.arange(experts, dtype=jnp.int32)[None, None, :]
    chosen = jnp.sum(jnp.where(picks, logits[:, None, :], 0.0), axis=-1)
    raised = jnp.exp(chosen)
    route_weights = raised / jnp.sum(raised, axis=-1, keepdims=True)
    capacity = 2 * ((5 * tokens * topk + 8 * experts - 1) // (8 * experts))
    owners = 2 * experts
    half_cap = capacity // 2
    flat_ids = chosen_ids.reshape(-1)
    pairs = flat_ids.shape[0]
    onehot = (flat_ids[:, None] == jnp.arange(experts, dtype=jnp.int32)[None, :]).astype(jnp.int32)
    slots = jnp.sum(onehot * (jnp.cumsum(onehot, axis=0) - 1), axis=1)
    dest = (slots % half_cap) * owners + 2 * flat_ids + slots // half_cap
    source_rows = jnp.arange(pairs, dtype=jnp.int32) // topk
    placed = jnp.any(
        dest.reshape(tokens, topk)[:, :, None] == jnp.arange(owners * half_cap, dtype=jnp.int32)[None, None, :],
        axis=1,
    ).astype(jnp.bfloat16)
    split = (
        jnp.einsum("tso,tw->osw", placed.reshape(tokens, half_cap, owners), normed, preferred_element_type=jnp.float32)
        .astype(jnp.bfloat16)
        .transpose(1, 0, 2)
    )
    in_weights = expert_in[0]
    out_weights = expert_out[0]
    half_width = out_weights.shape[0]
    received = lax.all_to_all(split, ("ctx", "grp"), split_axis=1, concat_axis=1, tiled=True)
    partner_rows = lax.ppermute(received, "grp", pair_perm)

    def expert_half(rows):
        pre = jnp.einsum("sow,wh->soh", rows, in_weights, preferred_element_type=jnp.float32)
        gate = pre[..., :half_width]
        upper = pre[..., half_width:]
        hidden = ((upper + 1.0) * gate * jax.nn.sigmoid(1.702 * gate)).astype(jnp.bfloat16)
        return jnp.einsum("soh,hw->sow", hidden, out_weights, preferred_element_type=jnp.float32).astype(
            jnp.bfloat16
        )

    own_part = expert_half(received)
    partner_part = expert_half(partner_rows)
    partner_back = lax.ppermute(partner_part, "grp", pair_perm)
    summed = (own_part.astype(jnp.float32) + partner_back.astype(jnp.float32)).astype(jnp.bfloat16)
    returned = lax.all_to_all(summed, ("ctx", "grp"), split_axis=1, concat_axis=1, tiled=True)
    order_dest = dest.reshape(tokens, topk).T.reshape(-1)
    picks = (order_dest[:, None] == jnp.arange(owners * half_cap, dtype=jnp.int32)[None, :]).astype(jnp.bfloat16)
    chosen_rows = jnp.einsum(
        "rso,sow->rw", picks.reshape(-1, half_cap, owners), returned, preferred_element_type=jnp.float32
    ).reshape(topk, tokens, width)
    mixture = mid_float
    for k in range(topk):
        mixture = mixture + chosen_rows[k] * route_weights[:, k:k + 1]
    final = mixture.astype(jnp.bfloat16)
    return (mid[None], final[None])


def solution(mesh):
    return jax.shard_map(
        body,
        mesh=mesh,
        in_specs=(
            P("grp", "ctx", None),
            P("grp", "ctx", None),
            P("grp", "ctx", None),
            P("grp", "ctx", None),
            P("grp", None),
            P(),
            P("ctx", None),
            P(),
            P(),
            P("grp", "ctx", None),
            P(("ctx", "grp"), None, None),
            P(("ctx", "grp"), None, None),
        ),
        out_specs=(P("grp", "ctx", None), P("grp", "ctx", None)),
        check_vma=False,
    )
```

```python
import math

import jax
import jax.numpy as jnp
from jax import lax
from jax.experimental import pallas as pl
from jax.experimental.pallas import tpu as pltpu
from jax.sharding import PartitionSpec as P

HEADS = 32
KVH = 8
HD = 64
CACHE_TK = 256


def flash_all(qpad, qpos, qstart, sink_rows, kv_all, cache_rows, bounds, steps, scale):
    pairs, rows, lanes = qpad.shape
    tokens = qpos.shape[0]
    sources, span, width = kv_all.shape
    stretch_rows = span - cache_rows
    cache_steps = cache_rows // CACHE_TK
    n_cache = sources * cache_steps
    v_base = width // 2
    reps = rows // tokens

    def block_of(j, s):
        return jnp.minimum(s[0] + j, s[1])

    def kernel(s_ref, q_ref, qpos_ref, qstart_ref, sink_ref, c_ref, t_ref, o_ref, m_sc, l_sc, acc_sc):
        j = pl.program_id(0)
        b = s_ref[0] + j

        @pl.when(j == 0)
        def _():
            m_sc[...] = sink_ref[...]
            l_sc[...] = jnp.zeros_like(l_sc)
            acc_sc[...] = jnp.zeros_like(acc_sc)

        def step(kv_ref, first, count, masked):
            if masked:
                kpos = first + lax.broadcasted_iota(jnp.int32, (1, count), 1)
                allowed = ((kpos <= qpos_ref[...]) & (kpos >= qstart_ref[...]))[None]
            for p in range(pairs):
                keys = kv_ref[:, p * lanes:(p + 1) * lanes]
                values = kv_ref[:, v_base + p * lanes:v_base + (p + 1) * lanes]
                s = lax.dot_general(
                    q_ref[p], keys, (((1,), (1,)), ((), ())), preferred_element_type=jnp.float32
                ) * scale
                m_prev = m_sc[p]
                if masked:
                    s3 = s.reshape(reps, tokens, count)
                    top = jnp.max(jnp.where(allowed, s3, -jnp.inf), axis=2, keepdims=True).reshape(rows, 1)
                    m_new = jnp.maximum(m_prev, top)
                    e3 = jnp.exp(s3 - m_new.reshape(reps, tokens, 1))
                    w = jnp.where(allowed, e3, 0.0).reshape(rows, count)
                else:
                    m_new = jnp.maximum(m_prev, jnp.max(s, axis=1, keepdims=True))
                    w = jnp.exp(s - m_new)
                shrink = jnp.exp(m_prev - m_new)
                l_sc[p] = l_sc[p] * shrink + jnp.sum(w, axis=1, keepdims=True)
                acc_sc[p] = acc_sc[p] * shrink + jnp.dot(
                    w.astype(jnp.bfloat16), values, preferred_element_type=jnp.float32
                )
                m_sc[p] = m_new

        live = b <= s_ref[1]

        def branch(kv_ref, first, count):
            inside = (first >= s_ref[3]) & (first + count - 1 <= s_ref[2])

            @pl.when(inside)
            def _():
                step(kv_ref, first, count, False)

            @pl.when(jnp.logical_not(inside))
            def _():
                step(kv_ref, first, count, True)

        @pl.when(live & (b < n_cache))
        def _():
            branch(c_ref, b * CACHE_TK, CACHE_TK)

        @pl.when(live & (b >= n_cache))
        def _():
            branch(t_ref, sources * cache_rows + (b - n_cache) * stretch_rows, stretch_rows)

        @pl.when(j == pl.num_programs(0) - 1)
        def _():
            denom = l_sc[...] + jnp.exp(sink_ref[...] - m_sc[...])
            o_ref[...] = (acc_sc[...] / denom).astype(o_ref.dtype)

    def cache_map(j, s):
        c = jnp.minimum(block_of(j, s), n_cache - 1)
        return (c // cache_steps, c % cache_steps, 0)

    def stretch_map(j, s):
        return (jnp.maximum(block_of(j, s) - n_cache, 0), cache_rows // stretch_rows, 0)

    grid_spec = pltpu.PrefetchScalarGridSpec(
        num_scalar_prefetch=1,
        grid=(steps,),
        in_specs=[
            pl.BlockSpec((pairs, rows, lanes), lambda j, s: (0, 0, 0)),
            pl.BlockSpec((tokens, 1), lambda j, s: (0, 0)),
            pl.BlockSpec((tokens, 1), lambda j, s: (0, 0)),
            pl.BlockSpec((pairs, rows, 1), lambda j, s: (0, 0, 0)),
            pl.BlockSpec((None, CACHE_TK, width), cache_map),
            pl.BlockSpec((None, stretch_rows, width), stretch_map),
        ],
        out_specs=pl.BlockSpec((pairs, rows, lanes), lambda j, s: (0, 0, 0)),
        scratch_shapes=[
            pltpu.VMEM((pairs, rows, 1), jnp.float32),
            pltpu.VMEM((pairs, rows, 1), jnp.float32),
            pltpu.VMEM((pairs, rows, lanes), jnp.float32),
        ],
    )
    keys = sources * span // 2
    return pl.pallas_call(
        kernel,
        grid_spec=grid_spec,
        out_shape=jax.ShapeDtypeStruct((pairs, rows, lanes), jnp.bfloat16),
        compiler_params=pltpu.CompilerParams(
            dimension_semantics=("arbitrary",), vmem_limit_bytes=48 * 1024 * 1024
        ),
        cost_estimate=pl.CostEstimate(
            flops=4 * pairs * rows * lanes * keys,
            transcendentals=pairs * rows * keys,
            bytes_accessed=kv_all.size + 4 * qpad.size,
        ),
    )(bounds, qpad, qpos, qstart, sink_rows, kv_all, kv_all)


def block_index(position, sources, cache_rows, stretch_rows):
    cache_end = sources * cache_rows
    return jnp.where(
        position < cache_end,
        position // CACHE_TK,
        sources * (cache_rows // CACHE_TK) + (position - cache_end) // stretch_rows,
    )


def attention(queries_local, kv_all, cache_rows, sinks, query_pos, query_start, longest):
    tokens = queries_local.shape[0]
    groups = HEADS // KVH
    pairs = KVH // 2
    sources, span, _ = kv_all.shape
    stretch_rows = span - cache_rows
    q6 = queries_local.reshape(tokens, pairs, 2, groups, HD).transpose(1, 2, 3, 0, 4)
    zeros = jnp.zeros_like(q6[:, 0])
    qpad = jnp.stack(
        [jnp.concatenate([q6[:, 0], zeros], axis=-1), jnp.concatenate([zeros, q6[:, 1]], axis=-1)], axis=1
    ).reshape(pairs, 2 * groups * tokens, 2 * HD)
    rows = 2 * groups * tokens
    sink_rows = jnp.repeat(sinks.reshape(pairs, 2 * groups), tokens, axis=1).reshape(pairs, rows, 1)
    first = block_index(query_start[0], sources, cache_rows, stretch_rows)
    last = block_index(query_pos[-1], sources, cache_rows, stretch_rows)
    bounds = jnp.stack([first, last, query_pos[0], query_start[-1]]).astype(jnp.int32)
    cache_end = sources * cache_rows

    def static_block(position):
        if position < cache_end:
            return position // CACHE_TK
        return sources * (cache_rows // CACHE_TK) + (position - cache_end) // stretch_rows

    steps = 1
    for device in range(sources):
        low_q = cache_end + device * tokens
        high_q = low_q + tokens - 1
        low = max(0, low_q - longest + 1)
        blocks = static_block(high_q) - static_block(low) + 1
        steps = max(steps, blocks)
    out = flash_all(
        qpad, query_pos.reshape(tokens, 1), query_start.reshape(tokens, 1), sink_rows, kv_all, cache_rows,
        bounds, steps, 1.0 / math.sqrt(HD),
    )
    o6 = out.reshape(pairs, 2, groups, tokens, 2, HD)
    picked = jnp.stack([o6[:, 0, :, :, 0], o6[:, 1, :, :, 1]], axis=1)
    return picked.transpose(3, 0, 1, 2, 4).reshape(tokens, HEADS * HD)


def doc_index(positions, lengths):
    ends = jnp.cumsum(lengths)
    return jnp.sum((positions[:, None] >= ends[None, :]).astype(jnp.int32), axis=1)


def gated_act(pre, half_width):
    gate = pre[:, :half_width]
    upper = pre[:, half_width:]
    return ((upper + 1.0) * gate * jax.nn.sigmoid(1.702 * gate)).astype(jnp.bfloat16)


def body(
    residual,
    queries,
    stretch_kv,
    cache_kv,
    doc_lengths,
    sinks,
    out_proj,
    norm_gain,
    router,
    expert_ids,
    expert_in,
    expert_out,
):
    tokens = residual.shape[1]
    width = residual.shape[2]
    cache_rows = cache_kv.shape[1]
    kv_cols = stretch_kv.shape[2] // 2
    groups = HEADS // KVH
    ctx_count = lax.axis_size("ctx")
    ctx_here = lax.axis_index("ctx")
    stretch_base = cache_rows * ctx_count
    span = cache_rows + tokens
    query_pos = stretch_base + ctx_here * tokens + jnp.arange(tokens, dtype=jnp.int32)
    lengths = doc_lengths[0]
    ends = jnp.cumsum(lengths)
    query_start = jnp.max(
        jnp.where(ends[None, :] <= query_pos[:, None], ends[None, :], 0), axis=1
    ).astype(jnp.int32)
    local_kv = jnp.concatenate([cache_kv[0], stretch_kv[0]], axis=0)
    kv_all = lax.all_gather(local_kv, "ctx", axis=0, tiled=False)
    attended = attention(queries[0], kv_all, cache_rows, sinks, query_pos, query_start, span * ctx_count // 2)
    grp_here = lax.axis_index("grp")
    parity = grp_here % 2
    grp_count = lax.axis_size("grp")
    pair_perm = [(g, g ^ 1) for g in range(grp_count)]
    head_rows = out_proj.shape[0] // 2
    proj_half = lax.all_gather(
        lax.dynamic_slice_in_dim(out_proj, parity * head_rows, head_rows, 0), "ctx", axis=0, tiled=True
    )
    by_parity = attended.reshape(tokens, HEADS // 2, 2, HD)
    mine = jnp.where(parity == 0, by_parity[:, :, 0], by_parity[:, :, 1]).reshape(tokens, -1)
    theirs_cols = jnp.where(parity == 0, by_parity[:, :, 1], by_parity[:, :, 0]).reshape(tokens, -1)
    partner_cols = lax.ppermute(theirs_cols, "grp", pair_perm)
    both = jnp.dot(
        jnp.concatenate([mine, partner_cols], axis=0), proj_half, preferred_element_type=jnp.float32
    )
    back = lax.ppermute(both[tokens:], "grp", pair_perm)
    projected = both[:tokens] + back
    mid = (residual[0].astype(jnp.float32) + projected).astype(jnp.bfloat16)
    mid_float = mid.astype(jnp.float32)
    normed = (
        mid_float
        * lax.rsqrt(jnp.mean(mid_float * mid_float, axis=-1, keepdims=True) + 1e-05)
        * norm_gain
    ).astype(jnp.bfloat16)
    logits = jnp.dot(normed, router, preferred_element_type=jnp.float32)
    experts = router.shape[1]
    chosen_ids = expert_ids[0]
    topk = chosen_ids.shape[1]
    picks = chosen_ids[:, :, None] == jnp.arange(experts, dtype=jnp.int32)[None, None, :]
    chosen = jnp.sum(jnp.where(picks, logits[:, None, :], 0.0), axis=-1)
    raised = jnp.exp(chosen)
    route_weights = raised / jnp.sum(raised, axis=-1, keepdims=True)
    capacity = 2 * ((5 * tokens * topk + 8 * experts - 1) // (8 * experts))
    owners = 2 * experts
    half_cap = capacity // 2
    flat_ids = chosen_ids.reshape(-1)
    pairs = flat_ids.shape[0]
    onehot = (flat_ids[:, None] == jnp.arange(experts, dtype=jnp.int32)[None, :]).astype(jnp.int32)
    slots = jnp.sum(onehot * (jnp.cumsum(onehot, axis=0) - 1), axis=1)
    dest = (slots % half_cap) * owners + 2 * flat_ids + slots // half_cap
    source_rows = jnp.arange(pairs, dtype=jnp.int32) // topk
    placed = jnp.any(
        dest.reshape(tokens, topk)[:, :, None] == jnp.arange(owners * half_cap, dtype=jnp.int32)[None, None, :],
        axis=1,
    ).astype(jnp.bfloat16)
    split = (
        jnp.einsum("tso,tw->osw", placed.reshape(tokens, half_cap, owners), normed, preferred_element_type=jnp.float32)
        .astype(jnp.bfloat16)
        .transpose(1, 0, 2)
    )
    in_weights = expert_in[0]
    out_weights = expert_out[0]
    half_width = out_weights.shape[0]
    received = lax.all_to_all(split, ("ctx", "grp"), split_axis=1, concat_axis=1, tiled=True)
    partner_rows = lax.ppermute(received, "grp", pair_perm)

    def expert_half(rows):
        pre = jnp.einsum("sow,wh->soh", rows, in_weights, preferred_element_type=jnp.float32)
        gate = pre[..., :half_width]
        upper = pre[..., half_width:]
        hidden = ((upper + 1.0) * gate * jax.nn.sigmoid(1.702 * gate)).astype(jnp.bfloat16)
        return jnp.einsum("soh,hw->sow", hidden, out_weights, preferred_element_type=jnp.float32).astype(
            jnp.bfloat16
        )

    def expert_hidden(rows):
        pre = jnp.einsum("sow,wh->soh", rows, in_weights, preferred_element_type=jnp.float32)
        gate = pre[..., :half_width]
        upper = pre[..., half_width:]
        return ((upper + 1.0) * gate * jax.nn.sigmoid(1.702 * gate)).astype(jnp.bfloat16)

    def expert_down(hidden):
        return jnp.einsum("soh,hw->sow", hidden, out_weights, preferred_element_type=jnp.float32).astype(
            jnp.bfloat16
        )

    own_hidden = expert_hidden(received)
    own_hidden, partner_rows = lax.optimization_barrier((own_hidden, partner_rows))
    partner_part = expert_down(expert_hidden(partner_rows))
    partner_back = lax.ppermute(partner_part, "grp", pair_perm)
    own_part = lax.optimization_barrier(expert_down(own_hidden))
    summed = (own_part.astype(jnp.float32) + partner_back.astype(jnp.float32)).astype(jnp.bfloat16)
    returned = lax.all_to_all(summed, ("ctx", "grp"), split_axis=1, concat_axis=1, tiled=True)
    order_dest = dest.reshape(tokens, topk).T.reshape(-1)
    picks = (order_dest[:, None] == jnp.arange(owners * half_cap, dtype=jnp.int32)[None, :]).astype(jnp.bfloat16)
    chosen_rows = jnp.einsum(
        "rso,sow->rw", picks.reshape(-1, half_cap, owners), returned, preferred_element_type=jnp.float32
    ).reshape(topk, tokens, width)
    mixture = mid_float
    for k in range(topk):
        mixture = mixture + chosen_rows[k] * route_weights[:, k:k + 1]
    final = mixture.astype(jnp.bfloat16)
    return (mid[None], final[None])


def solution(mesh):
    return jax.shard_map(
        body,
        mesh=mesh,
        in_specs=(
            P("grp", "ctx", None),
            P("grp", "ctx", None),
            P("grp", "ctx", None),
            P("grp", "ctx", None),
            P("grp", None),
            P(),
            P("ctx", None),
            P(),
            P(),
            P("grp", "ctx", None),
            P(("ctx", "grp"), None, None),
            P(("ctx", "grp"), None, None),
        ),
        out_specs=(P("grp", "ctx", None), P("grp", "ctx", None)),
        check_vma=False,
    )
```

```python
import math

import jax
import jax.numpy as jnp
from jax import lax
from jax.experimental import pallas as pl
from jax.experimental.pallas import tpu as pltpu
from jax.sharding import PartitionSpec as P

HEADS = 32
KVH = 8
HD = 64
CACHE_TK = 256


def flash_all(qpad, qpos, qstart, sink_rows, kv_all, cache_rows, bounds, steps, scale):
    pairs, rows, lanes = qpad.shape
    tokens = qpos.shape[0]
    sources, span, width = kv_all.shape
    stretch_rows = span - cache_rows
    cache_steps = cache_rows // CACHE_TK
    n_cache = sources * cache_steps
    v_base = width // 2
    reps = rows // tokens

    def block_of(j, s):
        return jnp.minimum(s[0] + j, s[1])

    def kernel(s_ref, q_ref, qpos_ref, qstart_ref, sink_ref, c_ref, t_ref, o_ref, m_sc, l_sc, acc_sc):
        j = pl.program_id(0)
        b = s_ref[0] + j

        @pl.when(j == 0)
        def _():
            m_sc[...] = sink_ref[...]
            l_sc[...] = jnp.zeros_like(l_sc)
            acc_sc[...] = jnp.zeros_like(acc_sc)

        def step(kv_ref, first, count, masked):
            if masked:
                kpos = first + lax.broadcasted_iota(jnp.int32, (1, count), 1)
                allowed = ((kpos <= qpos_ref[...]) & (kpos >= qstart_ref[...]))[None]
            for p in range(pairs):
                keys = kv_ref[:, p * lanes:(p + 1) * lanes]
                values = kv_ref[:, v_base + p * lanes:v_base + (p + 1) * lanes]
                s = lax.dot_general(
                    q_ref[p], keys, (((1,), (1,)), ((), ())), preferred_element_type=jnp.float32
                ) * scale
                m_prev = m_sc[p]
                if masked:
                    s3 = s.reshape(reps, tokens, count)
                    top = jnp.max(jnp.where(allowed, s3, -jnp.inf), axis=2, keepdims=True).reshape(rows, 1)
                    m_new = jnp.maximum(m_prev, top)
                    e3 = jnp.exp(s3 - m_new.reshape(reps, tokens, 1))
                    w = jnp.where(allowed, e3, 0.0).reshape(rows, count)
                else:
                    m_new = jnp.maximum(m_prev, jnp.max(s, axis=1, keepdims=True))
                    w = jnp.exp(s - m_new)
                shrink = jnp.exp(m_prev - m_new)
                l_sc[p] = l_sc[p] * shrink + jnp.sum(w, axis=1, keepdims=True)
                acc_sc[p] = acc_sc[p] * shrink + jnp.dot(
                    w.astype(jnp.bfloat16), values, preferred_element_type=jnp.float32
                )
                m_sc[p] = m_new

        live = b <= s_ref[1]

        def branch(kv_ref, first, count):
            inside = (first >= s_ref[3]) & (first + count - 1 <= s_ref[2])

            @pl.when(inside)
            def _():
                step(kv_ref, first, count, False)

            @pl.when(jnp.logical_not(inside))
            def _():
                step(kv_ref, first, count, True)

        @pl.when(live & (b < n_cache))
        def _():
            branch(c_ref, b * CACHE_TK, CACHE_TK)

        @pl.when(live & (b >= n_cache))
        def _():
            branch(t_ref, sources * cache_rows + (b - n_cache) * stretch_rows, stretch_rows)

        @pl.when(j == pl.num_programs(0) - 1)
        def _():
            denom = l_sc[...] + jnp.exp(sink_ref[...] - m_sc[...])
            o_ref[...] = (acc_sc[...] / denom).astype(o_ref.dtype)

    def cache_map(j, s):
        c = jnp.minimum(block_of(j, s), n_cache - 1)
        return (c // cache_steps, c % cache_steps, 0)

    def stretch_map(j, s):
        return (jnp.maximum(block_of(j, s) - n_cache, 0), cache_rows // stretch_rows, 0)

    grid_spec = pltpu.PrefetchScalarGridSpec(
        num_scalar_prefetch=1,
        grid=(steps,),
        in_specs=[
            pl.BlockSpec((pairs, rows, lanes), lambda j, s: (0, 0, 0)),
            pl.BlockSpec((tokens, 1), lambda j, s: (0, 0)),
            pl.BlockSpec((tokens, 1), lambda j, s: (0, 0)),
            pl.BlockSpec((pairs, rows, 1), lambda j, s: (0, 0, 0)),
            pl.BlockSpec((None, CACHE_TK, width), cache_map),
            pl.BlockSpec((None, stretch_rows, width), stretch_map),
        ],
        out_specs=pl.BlockSpec((pairs, rows, lanes), lambda j, s: (0, 0, 0)),
        scratch_shapes=[
            pltpu.VMEM((pairs, rows, 1), jnp.float32),
            pltpu.VMEM((pairs, rows, 1), jnp.float32),
            pltpu.VMEM((pairs, rows, lanes), jnp.float32),
        ],
    )
    keys = sources * span // 2
    return pl.pallas_call(
        kernel,
        grid_spec=grid_spec,
        out_shape=jax.ShapeDtypeStruct((pairs, rows, lanes), jnp.bfloat16),
        compiler_params=pltpu.CompilerParams(
            dimension_semantics=("arbitrary",), vmem_limit_bytes=48 * 1024 * 1024
        ),
        cost_estimate=pl.CostEstimate(
            flops=4 * pairs * rows * lanes * keys,
            transcendentals=pairs * rows * keys,
            bytes_accessed=kv_all.size + 4 * qpad.size,
        ),
    )(bounds, qpad, qpos, qstart, sink_rows, kv_all, kv_all)


def block_index(position, sources, cache_rows, stretch_rows):
    cache_end = sources * cache_rows
    return jnp.where(
        position < cache_end,
        position // CACHE_TK,
        sources * (cache_rows // CACHE_TK) + (position - cache_end) // stretch_rows,
    )


def attention(queries_local, kv_all, cache_rows, sinks, query_pos, query_start, longest):
    tokens = queries_local.shape[0]
    groups = HEADS // KVH
    pairs = KVH // 2
    sources, span, _ = kv_all.shape
    stretch_rows = span - cache_rows
    q6 = queries_local.reshape(tokens, pairs, 2, groups, HD).transpose(1, 2, 3, 0, 4)
    zeros = jnp.zeros_like(q6[:, 0])
    qpad = jnp.stack(
        [jnp.concatenate([q6[:, 0], zeros], axis=-1), jnp.concatenate([zeros, q6[:, 1]], axis=-1)], axis=1
    ).reshape(pairs, 2 * groups * tokens, 2 * HD)
    rows = 2 * groups * tokens
    sink_rows = jnp.repeat(sinks.reshape(pairs, 2 * groups), tokens, axis=1).reshape(pairs, rows, 1)
    first = block_index(query_start[0], sources, cache_rows, stretch_rows)
    last = block_index(query_pos[-1], sources, cache_rows, stretch_rows)
    bounds = jnp.stack([first, last, query_pos[0], query_start[-1]]).astype(jnp.int32)
    cache_end = sources * cache_rows

    def static_block(position):
        if position < cache_end:
            return position // CACHE_TK
        return sources * (cache_rows // CACHE_TK) + (position - cache_end) // stretch_rows

    steps = 1
    for device in range(sources):
        low_q = cache_end + device * tokens
        high_q = low_q + tokens - 1
        low = max(0, low_q - longest + 1)
        blocks = static_block(high_q) - static_block(low) + 1
        steps = max(steps, blocks)
    out = flash_all(
        qpad, query_pos.reshape(tokens, 1), query_start.reshape(tokens, 1), sink_rows, kv_all, cache_rows,
        bounds, steps, 1.0 / math.sqrt(HD),
    )
    o6 = out.reshape(pairs, 2, groups, tokens, 2, HD)
    picked = jnp.stack([o6[:, 0, :, :, 0], o6[:, 1, :, :, 1]], axis=1)
    return picked.transpose(3, 0, 1, 2, 4).reshape(tokens, HEADS * HD)


def doc_index(positions, lengths):
    ends = jnp.cumsum(lengths)
    return jnp.sum((positions[:, None] >= ends[None, :]).astype(jnp.int32), axis=1)


def gated_act(pre, half_width):
    gate = pre[:, :half_width]
    upper = pre[:, half_width:]
    return ((upper + 1.0) * gate * jax.nn.sigmoid(1.702 * gate)).astype(jnp.bfloat16)


def body(
    residual,
    queries,
    stretch_kv,
    cache_kv,
    doc_lengths,
    sinks,
    out_proj,
    norm_gain,
    router,
    expert_ids,
    expert_in,
    expert_out,
):
    tokens = residual.shape[1]
    width = residual.shape[2]
    cache_rows = cache_kv.shape[1]
    kv_cols = stretch_kv.shape[2] // 2
    groups = HEADS // KVH
    ctx_count = lax.axis_size("ctx")
    ctx_here = lax.axis_index("ctx")
    stretch_base = cache_rows * ctx_count
    span = cache_rows + tokens
    query_pos = stretch_base + ctx_here * tokens + jnp.arange(tokens, dtype=jnp.int32)
    lengths = doc_lengths[0]
    ends = jnp.cumsum(lengths)
    query_start = jnp.max(
        jnp.where(ends[None, :] <= query_pos[:, None], ends[None, :], 0), axis=1
    ).astype(jnp.int32)
    local_kv = jnp.concatenate([cache_kv[0], stretch_kv[0]], axis=0)
    kv_all = lax.all_gather(local_kv, "ctx", axis=0, tiled=False)
    attended = attention(queries[0], kv_all, cache_rows, sinks, query_pos, query_start, span * ctx_count // 2)
    grp_here = lax.axis_index("grp")
    parity = grp_here % 2
    grp_count = lax.axis_size("grp")
    pair_perm = [(g, g ^ 1) for g in range(grp_count)]
    head_rows = out_proj.shape[0] // 2
    proj_half = lax.all_gather(
        lax.dynamic_slice_in_dim(out_proj, parity * head_rows, head_rows, 0), "ctx", axis=0, tiled=True
    )
    by_parity = attended.reshape(tokens, HEADS // 2, 2, HD)
    mine = jnp.where(parity == 0, by_parity[:, :, 0], by_parity[:, :, 1]).reshape(tokens, -1)
    theirs_cols = jnp.where(parity == 0, by_parity[:, :, 1], by_parity[:, :, 0]).reshape(tokens, -1)
    partner_cols = lax.ppermute(theirs_cols, "grp", pair_perm)
    both = jnp.dot(
        jnp.concatenate([mine, partner_cols], axis=0), proj_half, preferred_element_type=jnp.float32
    )
    back = lax.ppermute(both[tokens:], "grp", pair_perm)
    projected = both[:tokens] + back
    mid = (residual[0].astype(jnp.float32) + projected).astype(jnp.bfloat16)
    mid_float = mid.astype(jnp.float32)
    normed = (
        mid_float
        * lax.rsqrt(jnp.mean(mid_float * mid_float, axis=-1, keepdims=True) + 1e-05)
        * norm_gain
    ).astype(jnp.bfloat16)
    logits = jnp.dot(normed, router, preferred_element_type=jnp.float32)
    experts = router.shape[1]
    chosen_ids = expert_ids[0]
    topk = chosen_ids.shape[1]
    picks = chosen_ids[:, :, None] == jnp.arange(experts, dtype=jnp.int32)[None, None, :]
    chosen = jnp.sum(jnp.where(picks, logits[:, None, :], 0.0), axis=-1)
    raised = jnp.exp(chosen)
    route_weights = raised / jnp.sum(raised, axis=-1, keepdims=True)
    capacity = 2 * ((5 * tokens * topk + 8 * experts - 1) // (8 * experts))
    owners = 2 * experts
    half_cap = capacity // 2
    flat_ids = chosen_ids.reshape(-1)
    pairs = flat_ids.shape[0]
    onehot = (flat_ids[:, None] == jnp.arange(experts, dtype=jnp.int32)[None, :]).astype(jnp.int32)
    slots = jnp.sum(onehot * (jnp.cumsum(onehot, axis=0) - 1), axis=1)
    dest = (slots % half_cap) * owners + 2 * flat_ids + slots // half_cap
    source_rows = jnp.arange(pairs, dtype=jnp.int32) // topk
    placed = jnp.any(
        dest.reshape(tokens, topk)[:, :, None] == jnp.arange(owners * half_cap, dtype=jnp.int32)[None, None, :],
        axis=1,
    ).astype(jnp.bfloat16)
    split = (
        jnp.einsum("tso,tw->osw", placed.reshape(tokens, half_cap, owners), normed, preferred_element_type=jnp.float32)
        .astype(jnp.bfloat16)
        .transpose(1, 0, 2)
    )
    in_weights = expert_in[0]
    out_weights = expert_out[0]
    half_width = out_weights.shape[0]
    received = lax.all_to_all(split, ("ctx", "grp"), split_axis=1, concat_axis=1, tiled=True)
    partner_rows = lax.ppermute(received, "grp", pair_perm)

    def expert_half(rows):
        pre = jnp.einsum("sow,wh->soh", rows, in_weights, preferred_element_type=jnp.float32)
        gate = pre[..., :half_width]
        upper = pre[..., half_width:]
        hidden = ((upper + 1.0) * gate * jax.nn.sigmoid(1.702 * gate)).astype(jnp.bfloat16)
        return jnp.einsum("soh,hw->sow", hidden, out_weights, preferred_element_type=jnp.float32).astype(
            jnp.bfloat16
        )

    own_part = expert_half(received)
    partner_part = expert_half(partner_rows)
    partner_back = lax.ppermute(partner_part, "grp", pair_perm)
    summed = (own_part.astype(jnp.float32) + partner_back.astype(jnp.float32)).astype(jnp.bfloat16)
    returned = lax.all_to_all(summed, ("ctx", "grp"), split_axis=1, concat_axis=1, tiled=True)
    slot_ids = jnp.arange(owners * half_cap, dtype=jnp.int32)
    placed_weights = jnp.sum(
        jnp.where(dest.reshape(tokens, topk)[:, :, None] == slot_ids[None, None, :], route_weights[:, :, None], 0.0),
        axis=1,
    )
    mixture = mid_float + jnp.einsum(
        "tso,sow->tw",
        placed_weights.reshape(tokens, half_cap, owners),
        returned.astype(jnp.float32),
        precision=lax.Precision.HIGHEST,
        preferred_element_type=jnp.float32,
    )
    final = mixture.astype(jnp.bfloat16)
    return (mid[None], final[None])


def solution(mesh):
    return jax.shard_map(
        body,
        mesh=mesh,
        in_specs=(
            P("grp", "ctx", None),
            P("grp", "ctx", None),
            P("grp", "ctx", None),
            P("grp", "ctx", None),
            P("grp", None),
            P(),
            P("ctx", None),
            P(),
            P(),
            P("grp", "ctx", None),
            P(("ctx", "grp"), None, None),
            P(("ctx", "grp"), None, None),
        ),
        out_specs=(P("grp", "ctx", None), P("grp", "ctx", None)),
        check_vma=False,
    )
```
